32 devices in a mesh: seq: 16 (over z, y, x), head: 2 (over core).
Axes of the slice: x: 2, y: 2, z: 4, core: 2. Of those that a mesh axis runs over, the one named last changes fastest.
Arguments:
- query_raw: bfloat16 [4096, 8, 128], P('seq', 'head'), may hold values from -6 to 6
- key_raw: bfloat16 [4096, 8, 128], P('seq', 'head'), may hold values from -6 to 6
- value_raw: bfloat16 [4096, 8, 128], P('seq', 'head'), may hold values from -6 to 6
- out_gain: float32 [8, 128], P('head'), may hold values from 0.5 to 1.5
- out_grad: bfloat16 [4096, 8, 128], P('seq', 'head'), may hold values from -6 to 6
Outputs:
- normed_out: bfloat16 [4096, 8, 128], P('seq', 'head')
- query_grad: bfloat16 [4096, 8, 128], P('seq', 'head')
- key_grad: bfloat16 [4096, 8, 128], P('seq', 'head')
- value_grad: bfloat16 [4096, 8, 128], P('seq', 'head')
The draws below stay inside these ranges and needn't reach their ends.
All inputs are finite; a program needn't handle non-finite values.
Results may differ from the reference program's by a relative error of at most 0.0065.
Values sent between devices are 32-bit elements; how exact they have to be, the bound alone decides.
No kernel may reach another device: no remote copies, remote signals or barrier semaphores. Data moves between devices by JAX's collectives and lax.ppermute only.
A program may use at most 64 MiB of HBM per device.

```python
import jax
import jax.numpy as jnp
from jax import lax

DH = 128
GROUP = 256
TOKENS = 4096
HEADS = 8


def block_scale(rng, shape, cuts, smallest, high):
    level = 1.0
    for axis_at, parts in cuts:
        steps = jax.random.uniform(jax.random.fold_in(jax.random.fold_in(rng, 6), axis_at), (parts,), jnp.float32, smallest / len(cuts), high / len(cuts))
        level = level * jnp.repeat(jnp.exp(steps), shape[axis_at] // parts).reshape((-1,) + (1,) * (len(shape) - 1 - axis_at))
    return level


def centred(rng, shape, scale, limit, shards=(), kind=jnp.bfloat16):
    drawn = jax.random.normal(rng, shape, jnp.float32) * scale
    if len(shards) > 0:
        drawn = block_scale(rng, shape, shards, -0.22, 0.18) * drawn
    return jnp.clip(drawn, min=-limit, max=limit).astype(kind)


def setup_inputs(seed: int = 0) -> dict:
    streams_of = jax.random.split(jax.random.key(seed), 6)
    return {
        "query_raw": centred(streams_of[0], (TOKENS, HEADS, DH), 1.0, 6.0, ((0, 16), (1, 2))),
        "key_raw": centred(streams_of[1], (TOKENS, HEADS, DH), 1.0, 6.0, ((0, 16), (1, 2))),
        "value_raw": centred(streams_of[2], (TOKENS, HEADS, DH), 1.0, 6.0, ((0, 16), (1, 2))),
        "out_gain": jnp.clip(1.0 + 0.1 * jax.random.normal(streams_of[3], (HEADS, DH), jnp.float32), 0.5, 1.5),
        "out_grad": centred(streams_of[4], (TOKENS, HEADS, DH), 1.0, 6.0, ((0, 16), (1, 2))),
    }


def silu_grad(raw):
    sigma = jax.nn.sigmoid(raw)
    return sigma * (1.0 + raw * (1.0 - sigma))

def causal_mask(length):
    rows = lax.broadcasted_iota(jnp.int32, (length, length), 0)
    cols = lax.broadcasted_iota(jnp.int32, (length, length), 1)
    return cols <= rows

def round_trip(value):
    return lax.optimization_barrier(value.astype(jnp.bfloat16)).astype(jnp.float32)

def reference(query_raw, key_raw, value_raw, out_gain, out_grad):
    blocks = TOKENS // GROUP
    blocked = (blocks, GROUP, HEADS, DH)
    query_act = jax.nn.silu(query_raw.astype(jnp.float32)).astype(jnp.bfloat16)
    key_act = jax.nn.silu(key_raw.astype(jnp.float32)).astype(jnp.bfloat16)
    query_blk = query_act.reshape(blocked)
    key_blk = key_act.reshape(blocked)
    value_blk = value_raw.reshape(blocked)
    grad_blk = out_grad.reshape(blocked)
    mask = causal_mask(GROUP)
    features = HEADS * DH
    gain_f = out_gain.astype(jnp.float32)

    def forward_step(state, block):
        query_c, key_c, value_c, grad_c = block
        query_f = query_c.astype(jnp.float32)
        key_f = key_c.astype(jnp.float32)
        value_f = value_c.astype(jnp.float32)
        scores = jnp.einsum('thd,shd->hts', query_f, key_f)
        attn = round_trip(jnp.where(mask[None], scores, 0.0))
        state_b = round_trip(state)
        mixed = jnp.einsum('hts,she->the', attn, value_f) + jnp.einsum('thd,hde->the', query_f, state_b)
        grad_in = grad_c.astype(jnp.float32) * gain_f
        sq_total = lax.optimization_barrier(jnp.sum(mixed * mixed, axis=(1, 2)))
        cross_total = lax.optimization_barrier(jnp.sum(grad_in * mixed, axis=(1, 2)))
        inv_rms = lax.rsqrt(sq_total / features + 1e-06)
        normed = (mixed * inv_rms[:, None, None] * gain_f).astype(jnp.bfloat16)
        delta = (grad_in * inv_rms[:, None, None] - mixed * (cross_total * inv_rms ** 3 / features)[:, None, None]).astype(jnp.bfloat16)
        state = state + jnp.einsum('shd,she->hde', key_f, value_f)
        return (state, (normed, delta, state_b.astype(jnp.bfloat16)))
    start = jnp.zeros((HEADS, DH, DH), jnp.float32)
    unused, (normed, delta, states) = lax.scan(forward_step, start, (query_blk, key_blk, value_blk, grad_blk))
    query_raw_blk = query_raw.reshape(blocked)
    key_raw_blk = key_raw.reshape(blocked)

    def backward_step(grad_state, block):
        query_c, key_c, value_c, delta_c, state_c, qraw_c, kraw_c = block
        query_f = query_c.astype(jnp.float32)
        key_f = key_c.astype(jnp.float32)
        value_f = value_c.astype(jnp.float32)
        delta_f = delta_c.astype(jnp.float32)
        state_f = state_c.astype(jnp.float32)
        grad_b = round_trip(grad_state)
        scores = jnp.einsum('thd,shd->hts', query_f, key_f)
        attn = round_trip(jnp.where(mask[None], scores, 0.0))
        bscore = round_trip(jnp.where(mask[None], jnp.einsum('the,she->hts', delta_f, value_f), 0.0))
        dquery = jnp.einsum('hts,shd->thd', bscore, key_f) + jnp.einsum('the,hde->thd', delta_f, state_f)
        dkey = jnp.einsum('hts,thd->shd', bscore, query_f) + jnp.einsum('she,hde->shd', value_f, grad_b)
        dvalue = jnp.einsum('hts,the->she', attn, delta_f) + jnp.einsum('shd,hde->she', key_f, grad_b)
        query_out = (dquery * silu_grad(qraw_c.astype(jnp.float32))).astype(jnp.bfloat16)
        key_out = (dkey * silu_grad(kraw_c.astype(jnp.float32))).astype(jnp.bfloat16)
        grad_state = grad_state + jnp.einsum('thd,the->hde', query_f, delta_f)
        return (grad_state, (query_out, key_out, dvalue.astype(jnp.bfloat16)))
    unused_two, (query_grad, key_grad, value_grad) = lax.scan(backward_step, start, (query_blk, key_blk, value_blk, delta, states, query_raw_blk, key_raw_blk), reverse=True)
    whole = (TOKENS, HEADS, DH)
    return (normed.reshape(whole), query_grad.reshape(whole), key_grad.reshape(whole), value_grad.reshape(whole))
```

```python
import jax
import jax.numpy as jnp
from jax import lax
from jax.sharding import PartitionSpec as P

GROUP = 256


def from_behind(shard, axis, by):
    count = lax.axis_size(axis)
    pairs = [(i, i + by) for i in range(count) if 0 <= i + by < count]
    return lax.ppermute(shard, axis, pairs)


def silu_grad(raw):
    sigma = jax.nn.sigmoid(raw)
    return sigma * (1.0 + raw * (1.0 - sigma))


def causal_mask(length):
    rows = lax.broadcasted_iota(jnp.int32, (length, length), 0)
    cols = lax.broadcasted_iota(jnp.int32, (length, length), 1)
    return cols <= rows


def exclusive_scan(own_total, reverse):
    count = lax.axis_size("seq")
    flat = own_total.reshape(-1)
    size = flat.shape[0]
    chunk = -(-size // count)
    flat = jnp.pad(flat, (0, chunk * count - size))
    gathered = lax.all_to_all(flat.reshape(count, chunk), "seq", 0, 0, tiled=True)
    zero = jnp.zeros((1, chunk), gathered.dtype)
    if reverse:
        later = jnp.flip(jnp.cumsum(jnp.flip(gathered[1:], 0), axis=0), 0)
        prefix = jnp.concatenate([later, zero], axis=0)
    else:
        prefix = jnp.concatenate([zero, jnp.cumsum(gathered[:-1], axis=0)], axis=0)
    spread = lax.all_to_all(prefix, "seq", 0, 0, tiled=True)
    return spread.reshape(-1)[:size].reshape(own_total.shape)


def lower_sum(own_total):
    return exclusive_scan(own_total, False)


def upper_sum(own_total):
    return exclusive_scan(own_total, True)


def body(query_raw, key_raw, value_raw, out_gain, out_grad):
    tok_rows, head_count, width = query_raw.shape
    blocks = tok_rows // GROUP
    blocked = (blocks, GROUP, head_count, width)
    query_act = jax.nn.silu(query_raw.astype(jnp.float32)).astype(jnp.bfloat16).reshape(blocked)
    key_act = jax.nn.silu(key_raw.astype(jnp.float32)).astype(jnp.bfloat16).reshape(blocked)
    value_blk = value_raw.reshape(blocked)
    mask = causal_mask(GROUP)[None, None]
    block_kv = jnp.einsum("cshd,cshe->chde", key_act, value_blk, preferred_element_type=jnp.float32)
    own_total = jnp.sum(block_kv, axis=0)
    before = lower_sum(own_total)
    state_b = (before[None] + (jnp.cumsum(block_kv, axis=0) - block_kv)).astype(jnp.bfloat16)
    scores = jnp.einsum("cthd,cshd->chts", query_act, key_act, preferred_element_type=jnp.float32)
    attn = jnp.where(mask, scores, 0.0).astype(jnp.bfloat16)
    mixed = jnp.einsum("chts,cshe->cthe", attn, value_blk, preferred_element_type=jnp.float32)
    mixed = mixed + jnp.einsum(
        "cthd,chde->cthe", query_act, state_b, preferred_element_type=jnp.float32
    )
    mixed = mixed.reshape(tok_rows, head_count, width)
    grad_in = out_grad.astype(jnp.float32) * out_gain
    sq_part = jnp.sum(mixed * mixed, axis=(1, 2))
    cross_part = jnp.sum(grad_in * mixed, axis=(1, 2))
    sq_total, cross_total = lax.psum((sq_part, cross_part), "head")
    features = head_count * width * lax.axis_size("head")
    inv_rms = lax.rsqrt(sq_total / features + 1e-06)
    normed_out = (mixed * inv_rms[:, None, None] * out_gain).astype(jnp.bfloat16)
    delta = (
        grad_in * inv_rms[:, None, None]
        - mixed * (cross_total * inv_rms**3 / features)[:, None, None]
    ).astype(jnp.bfloat16)
    delta_blk = delta.reshape(blocked)
    block_grad = jnp.einsum(
        "cthd,cthe->chde", query_act, delta_blk, preferred_element_type=jnp.float32
    )
    own_grad = jnp.sum(block_grad, axis=0)
    after = upper_sum(own_grad)
    local_after = jnp.flip(jnp.cumsum(jnp.flip(block_grad, 0), axis=0), 0) - block_grad
    grad_state = (after[None] + local_after).astype(jnp.bfloat16)
    bscore = jnp.einsum("cthe,cshe->chts", delta_blk, value_blk, preferred_element_type=jnp.float32)
    bscore = jnp.where(mask, bscore, 0.0).astype(jnp.bfloat16)
    dquery = jnp.einsum("chts,cshd->cthd", bscore, key_act, preferred_element_type=jnp.float32)
    dquery = dquery + jnp.einsum(
        "cthe,chde->cthd", delta_blk, state_b, preferred_element_type=jnp.float32
    )
    dkey = jnp.einsum("chts,cthd->cshd", bscore, query_act, preferred_element_type=jnp.float32)
    dkey = dkey + jnp.einsum(
        "cshe,chde->cshd", value_blk, grad_state, preferred_element_type=jnp.float32
    )
    dvalue = jnp.einsum("chts,cthe->cshe", attn, delta_blk, preferred_element_type=jnp.float32)
    dvalue = dvalue + jnp.einsum(
        "cshd,chde->cshe", key_act, grad_state, preferred_element_type=jnp.float32
    )
    whole = (tok_rows, head_count, width)
    query_grad = (dquery.reshape(whole) * silu_grad(query_raw.astype(jnp.float32))).astype(
        jnp.bfloat16
    )
    key_grad = (dkey.reshape(whole) * silu_grad(key_raw.astype(jnp.float32))).astype(jnp.bfloat16)
    value_grad = dvalue.reshape(whole).astype(jnp.bfloat16)
    return (normed_out, query_grad, key_grad, value_grad)


def solution(mesh):
    in_specs = (
        P("seq", "head", None),
        P("seq", "head", None),
        P("seq", "head", None),
        P("head", None),
        P("seq", "head", None),
    )
    out_specs = (
        P("seq", "head", None),
        P("seq", "head", None),
        P("seq", "head", None),
        P("seq", "head", None),
    )
    return jax.shard_map(body, mesh=mesh, in_specs=in_specs, out_specs=out_specs, check_vma=False)
```

```python
import jax
import jax.numpy as jnp
from jax import lax
from jax.sharding import PartitionSpec as P

GROUP = 256


def from_behind(shard, axis, by):
    count = lax.axis_size(axis)
    pairs = [(i, i + by) for i in range(count) if 0 <= i + by < count]
    return lax.ppermute(shard, axis, pairs)


def silu_grad(raw):
    sigma = jax.nn.sigmoid(raw)
    return sigma * (1.0 + raw * (1.0 - sigma))


def causal_mask(length):
    rows = lax.broadcasted_iota(jnp.int32, (length, length), 0)
    cols = lax.broadcasted_iota(jnp.int32, (length, length), 1)
    return cols <= rows


def exclusive_scan(own_total, reverse):
    count = lax.axis_size("seq")
    width = own_total.shape[-1]
    rows = own_total.reshape(-1, width)
    size = rows.shape[0]
    chunk = -(-size // count)
    rows = jnp.pad(rows, ((0, chunk * count - size), (0, 0)))
    gathered = lax.all_to_all(rows.reshape(count, chunk, width), "seq", 0, 0, tiled=True)
    inclusive = lax.cumsum(gathered, axis=0, reverse=reverse)
    prefix = inclusive - gathered
    spread = lax.all_to_all(prefix, "seq", 0, 0, tiled=True)
    return spread.reshape(-1, width)[:size].reshape(own_total.shape)


def lower_sum(own_total):
    return exclusive_scan(own_total, False)


def upper_sum(own_total):
    return exclusive_scan(own_total, True)


def body(query_raw, key_raw, value_raw, out_gain, out_grad):
    tok_rows, head_count, width = query_raw.shape
    blocks = tok_rows // GROUP
    blocked = (blocks, GROUP, head_count, width)
    query_act = jax.nn.silu(query_raw.astype(jnp.float32)).astype(jnp.bfloat16).reshape(blocked)
    key_act = jax.nn.silu(key_raw.astype(jnp.float32)).astype(jnp.bfloat16).reshape(blocked)
    value_blk = value_raw.reshape(blocked)
    mask = causal_mask(GROUP)[None, None]
    block_kv = jnp.einsum("cshd,cshe->chde", key_act, value_blk, preferred_element_type=jnp.float32)
    own_total = jnp.sum(block_kv, axis=0)
    before = lower_sum(own_total)
    state_b = (before[None] + (jnp.cumsum(block_kv, axis=0) - block_kv)).astype(jnp.bfloat16)
    scores = jnp.einsum("cthd,cshd->chts", query_act, key_act, preferred_element_type=jnp.float32)
    attn = jnp.where(mask, scores, 0.0).astype(jnp.bfloat16)
    mixed = jnp.einsum("chts,cshe->cthe", attn, value_blk, preferred_element_type=jnp.float32)
    mixed = mixed + jnp.einsum(
        "cthd,chde->cthe", query_act, state_b, preferred_element_type=jnp.float32
    )
    mixed = mixed.reshape(tok_rows, head_count, width)
    grad_in = out_grad.astype(jnp.float32) * out_gain
    sq_part = jnp.sum(mixed * mixed, axis=(1, 2))
    cross_part = jnp.sum(grad_in * mixed, axis=(1, 2))
    both = jnp.stack([sq_part, cross_part])
    both = both + lax.ppermute(both, "head", [(0, 1), (1, 0)])
    sq_total, cross_total = both[0], both[1]
    features = head_count * width * lax.axis_size("head")
    inv_rms = lax.rsqrt(sq_total / features + 1e-06)
    normed_out = (mixed * inv_rms[:, None, None] * out_gain).astype(jnp.bfloat16)
    delta = (
        grad_in * inv_rms[:, None, None]
        - mixed * (cross_total * inv_rms**3 / features)[:, None, None]
    ).astype(jnp.bfloat16)
    delta_blk = delta.reshape(blocked)
    block_grad = jnp.einsum(
        "cthd,cthe->chde", query_act, delta_blk, preferred_element_type=jnp.float32
    )
    own_grad = jnp.sum(block_grad, axis=0)
    after = upper_sum(own_grad)
    local_after = jnp.flip(jnp.cumsum(jnp.flip(block_grad, 0), axis=0), 0) - block_grad
    grad_state = (after[None] + local_after).astype(jnp.bfloat16)
    bscore = jnp.einsum("cthe,cshe->chts", delta_blk, value_blk, preferred_element_type=jnp.float32)
    bscore = jnp.where(mask, bscore, 0.0).astype(jnp.bfloat16)
    dquery = jnp.einsum("chts,cshd->cthd", bscore, key_act, preferred_element_type=jnp.float32)
    dquery = dquery + jnp.einsum(
        "cthe,chde->cthd", delta_blk, state_b, preferred_element_type=jnp.float32
    )
    dkey = jnp.einsum("chts,cthd->cshd", bscore, query_act, preferred_element_type=jnp.float32)
    dkey = dkey + jnp.einsum(
        "cshe,chde->cshd", value_blk, grad_state, preferred_element_type=jnp.float32
    )
    dvalue = jnp.einsum("chts,cthe->cshe", attn, delta_blk, preferred_element_type=jnp.float32)
    dvalue = dvalue + jnp.einsum(
        "cshd,chde->cshe", key_act, grad_state, preferred_element_type=jnp.float32
    )
    whole = (tok_rows, head_count, width)
    query_grad = (dquery.reshape(whole) * silu_grad(query_raw.astype(jnp.float32))).astype(
        jnp.bfloat16
    )
    key_grad = (dkey.reshape(whole) * silu_grad(key_raw.astype(jnp.float32))).astype(jnp.bfloat16)
    value_grad = dvalue.reshape(whole).astype(jnp.bfloat16)
    return (normed_out, query_grad, key_grad, value_grad)


def solution(mesh):
    in_specs = (
        P("seq", "head", None),
        P("seq", "head", None),
        P("seq", "head", None),
        P("head", None),
        P("seq", "head", None),
    )
    out_specs = (
        P("seq", "head", None),
        P("seq", "head", None),
        P("seq", "head", None),
        P("seq", "head", None),
    )
    return jax.shard_map(body, mesh=mesh, in_specs=in_specs, out_specs=out_specs, check_vma=False)
```

```python
import jax
import jax.numpy as jnp
from jax import lax
from jax.sharding import PartitionSpec as P

GROUP = 256


def from_behind(shard, axis, by):
    count = lax.axis_size(axis)
    pairs = [(i, i + by) for i in range(count) if 0 <= i + by < count]
    return lax.ppermute(shard, axis, pairs)


def silu_grad(raw):
    sigma = jax.nn.sigmoid(raw)
    return sigma * (1.0 + raw * (1.0 - sigma))


def causal_mask(length):
    rows = lax.broadcasted_iota(jnp.int32, (length, length), 0)
    cols = lax.broadcasted_iota(jnp.int32, (length, length), 1)
    return cols <= rows


def exclusive_scan(own_total, reverse):
    count = lax.axis_size("seq")
    width = own_total.shape[-1]
    rows = own_total.reshape(-1, width)
    size = rows.shape[0]
    chunk = -(-size // count)
    rows = jnp.pad(rows, ((0, chunk * count - size), (0, 0)))
    gathered = lax.all_to_all(rows.reshape(count, chunk, width), "seq", 0, 0, tiled=True)
    if count > 32:
        prefix = lax.cumsum(gathered, axis=0, reverse=reverse) - gathered
    else:
        order = range(count - 1, -1, -1) if reverse else range(count)
        running = jnp.zeros_like(gathered[0])
        parts = [None] * count
        for index in order:
            parts[index] = running
            running = running + gathered[index]
        prefix = jnp.stack(parts)
    spread = lax.all_to_all(prefix, "seq", 0, 0, tiled=True)
    return spread.reshape(-1, width)[:size].reshape(own_total.shape)


def lower_sum(own_total):
    return exclusive_scan(own_total, False)


def upper_sum(own_total):
    return exclusive_scan(own_total, True)


def body(query_raw, key_raw, value_raw, out_gain, out_grad):
    tok_rows, head_count, width = query_raw.shape
    blocks = tok_rows // GROUP
    blocked = (blocks, GROUP, head_count, width)
    query_act = jax.nn.silu(query_raw.astype(jnp.float32)).astype(jnp.bfloat16).reshape(blocked)
    key_act = jax.nn.silu(key_raw.astype(jnp.float32)).astype(jnp.bfloat16).reshape(blocked)
    value_blk = value_raw.reshape(blocked)
    mask = causal_mask(GROUP)[None, None]
    block_kv = jnp.einsum("cshd,cshe->chde", key_act, value_blk, preferred_element_type=jnp.float32)
    own_total = jnp.sum(block_kv, axis=0)
    before = lower_sum(own_total)
    state_b = (before[None] + (jnp.cumsum(block_kv, axis=0) - block_kv)).astype(jnp.bfloat16)
    scores = jnp.einsum("cthd,cshd->chts", query_act, key_act, preferred_element_type=jnp.float32)
    attn = jnp.where(mask, scores, 0.0).astype(jnp.bfloat16)
    mixed = jnp.einsum("chts,cshe->cthe", attn, value_blk, preferred_element_type=jnp.float32)
    mixed = mixed + jnp.einsum(
        "cthd,chde->cthe", query_act, state_b, preferred_element_type=jnp.float32
    )
    mixed = mixed.reshape(tok_rows, head_count, width)
    grad_in = out_grad.astype(jnp.float32) * out_gain
    sq_part = jnp.sum(mixed * mixed, axis=(1, 2))
    cross_part = jnp.sum(grad_in * mixed, axis=(1, 2))
    both = jnp.stack([sq_part, cross_part])
    both = both + lax.ppermute(both, "head", [(0, 1), (1, 0)])
    sq_total, cross_total = both[0], both[1]
    features = head_count * width * lax.axis_size("head")
    inv_rms = lax.rsqrt(sq_total / features + 1e-06)
    normed_out = (mixed * inv_rms[:, None, None] * out_gain).astype(jnp.bfloat16)
    delta = (
        grad_in * inv_rms[:, None, None]
        - mixed * (cross_total * inv_rms**3 / features)[:, None, None]
    ).astype(jnp.bfloat16)
    delta_blk = delta.reshape(blocked)
    block_grad = jnp.einsum(
        "cthd,cthe->chde", query_act, delta_blk, preferred_element_type=jnp.float32
    )
    own_grad = jnp.sum(block_grad, axis=0)
    after = upper_sum(own_grad)
    local_after = lax.cumsum(block_grad, axis=0, reverse=True) - block_grad
    grad_state = (after[None] + local_after).astype(jnp.bfloat16)
    bscore = jnp.einsum("cthe,cshe->chts", delta_blk, value_blk, preferred_element_type=jnp.float32)
    bscore = jnp.where(mask, bscore, 0.0).astype(jnp.bfloat16)
    dquery = jnp.einsum("chts,cshd->cthd", bscore, key_act, preferred_element_type=jnp.float32)
    dquery = dquery + jnp.einsum(
        "cthe,chde->cthd", delta_blk, state_b, preferred_element_type=jnp.float32
    )
    dkey = jnp.einsum("chts,cthd->cshd", bscore, query_act, preferred_element_type=jnp.float32)
    dkey = dkey + jnp.einsum(
        "cshe,chde->cshd", value_blk, grad_state, preferred_element_type=jnp.float32
    )
    dvalue = jnp.einsum("chts,cthe->cshe", attn, delta_blk, preferred_element_type=jnp.float32)
    dvalue = dvalue + jnp.einsum(
        "cshd,chde->cshe", key_act, grad_state, preferred_element_type=jnp.float32
    )
    whole = (tok_rows, head_count, width)
    query_grad = (dquery.reshape(whole) * silu_grad(query_raw.astype(jnp.float32))).astype(
        jnp.bfloat16
    )
    key_grad = (dkey.reshape(whole) * silu_grad(key_raw.astype(jnp.float32))).astype(jnp.bfloat16)
    value_grad = dvalue.reshape(whole).astype(jnp.bfloat16)
    return (normed_out, query_grad, key_grad, value_grad)


def solution(mesh):
    in_specs = (
        P("seq", "head", None),
        P("seq", "head", None),
        P("seq", "head", None),
        P("head", None),
        P("seq", "head", None),
    )
    out_specs = (
        P("seq", "head", None),
        P("seq", "head", None),
        P("seq", "head", None),
        P("seq", "head", None),
    )
    return jax.shard_map(body, mesh=mesh, in_specs=in_specs, out_specs=out_specs, check_vma=False)
```

```python
import jax
import jax.numpy as jnp
from jax import lax
from jax.sharding import PartitionSpec as P

GROUP = 256


def from_behind(shard, axis, by):
    count = lax.axis_size(axis)
    pairs = [(i, i + by) for i in range(count) if 0 <= i + by < count]
    return lax.ppermute(shard, axis, pairs)


def silu_grad(raw):
    sigma = jax.nn.sigmoid(raw)
    return sigma * (1.0 + raw * (1.0 - sigma))


def causal_mask(length):
    rows = lax.broadcasted_iota(jnp.int32, (length, length), 0)
    cols = lax.broadcasted_iota(jnp.int32, (length, length), 1)
    return cols <= rows


def exclusive_scan(own_total, reverse):
    count = lax.axis_size("seq")
    width = own_total.shape[-1]
    rows = own_total.reshape(-1, width)
    size = rows.shape[0]
    chunk = -(-size // count)
    rows = jnp.pad(rows, ((0, chunk * count - size), (0, 0)))
    gathered = lax.all_to_all(rows.reshape(count, chunk, width), "seq", 0, 0, tiled=True)
    inclusive = lax.cumsum(gathered, axis=0, reverse=reverse)
    prefix = inclusive - gathered
    spread = lax.all_to_all(prefix, "seq", 0, 0, tiled=True)
    return spread.reshape(-1, width)[:size].reshape(own_total.shape)


def lower_sum(own_total):
    return exclusive_scan(own_total, False)


def upper_sum(own_total):
    return exclusive_scan(own_total, True)


def mm(lhs, rhs, lhs_dim, rhs_dim):
    dims = (((lhs_dim,), (rhs_dim,)), ((), ()))
    return lax.dot_general(lhs, rhs, dims, preferred_element_type=jnp.float32)


def body(query_raw, key_raw, value_raw, out_gain, out_grad):
    tok_rows, head_count, width = query_raw.shape
    blocks = tok_rows // GROUP
    query_act = jax.nn.silu(query_raw.astype(jnp.float32)).astype(jnp.bfloat16)
    key_act = jax.nn.silu(key_raw.astype(jnp.float32)).astype(jnp.bfloat16)
    mask = causal_mask(GROUP)
    cells = [(c, h) for c in range(blocks) for h in range(head_count)]

    def cut(array, c, h):
        return array[c * GROUP:(c + 1) * GROUP, h, :]

    def join(parts):
        rows = [jnp.stack([parts[(c, h)] for h in range(head_count)], axis=1) for c in range(blocks)]
        return rows[0] if blocks == 1 else jnp.concatenate(rows, axis=0)

    block_kv = jnp.stack([
        jnp.stack([mm(cut(key_act, c, h), cut(value_raw, c, h), 0, 0) for h in range(head_count)])
        for c in range(blocks)
    ])
    own_total = jnp.sum(block_kv, axis=0)
    before = lower_sum(own_total)
    state_b = (before[None] + (jnp.cumsum(block_kv, axis=0) - block_kv)).astype(jnp.bfloat16)
    attn = {}
    mixed_parts = {}
    for c, h in cells:
        scores = mm(cut(query_act, c, h), cut(key_act, c, h), 1, 1)
        attn[c, h] = jnp.where(mask, scores, 0.0).astype(jnp.bfloat16)
        mixed_parts[c, h] = mm(attn[c, h], cut(value_raw, c, h), 1, 0) + mm(
            cut(query_act, c, h), state_b[c, h], 1, 0
        )
    mixed = join(mixed_parts)
    grad_in = out_grad.astype(jnp.float32) * out_gain
    sq_part = jnp.sum(mixed * mixed, axis=(1, 2))
    cross_part = jnp.sum(grad_in * mixed, axis=(1, 2))
    both = jnp.stack([sq_part, cross_part])
    both = both + lax.ppermute(both, "head", [(0, 1), (1, 0)])
    sq_total, cross_total = both[0], both[1]
    features = head_count * width * lax.axis_size("head")
    inv_rms = lax.rsqrt(sq_total / features + 1e-06)
    normed_out = (mixed * inv_rms[:, None, None] * out_gain).astype(jnp.bfloat16)
    delta = (
        grad_in * inv_rms[:, None, None]
        - mixed * (cross_total * inv_rms**3 / features)[:, None, None]
    ).astype(jnp.bfloat16)
    block_grad = jnp.stack([
        jnp.stack([mm(cut(query_act, c, h), cut(delta, c, h), 0, 0) for h in range(head_count)])
        for c in range(blocks)
    ])
    own_grad = jnp.sum(block_grad, axis=0)
    after = upper_sum(own_grad)
    local_after = lax.cumsum(block_grad, axis=0, reverse=True) - block_grad
    grad_state = (after[None] + local_after).astype(jnp.bfloat16)
    dq_parts, dk_parts, dv_parts = {}, {}, {}
    for c, h in cells:
        delta_c = cut(delta, c, h)
        value_c = cut(value_raw, c, h)
        bscore = jnp.where(mask, mm(delta_c, value_c, 1, 1), 0.0).astype(jnp.bfloat16)
        dq_parts[c, h] = mm(bscore, cut(key_act, c, h), 1, 0) + mm(delta_c, state_b[c, h], 1, 1)
        dk_parts[c, h] = mm(bscore, cut(query_act, c, h), 0, 0) + mm(value_c, grad_state[c, h], 1, 1)
        dv_parts[c, h] = mm(attn[c, h], delta_c, 0, 0) + mm(cut(key_act, c, h), grad_state[c, h], 1, 0)
    query_grad = (join(dq_parts) * silu_grad(query_raw.astype(jnp.float32))).astype(jnp.bfloat16)
    key_grad = (join(dk_parts) * silu_grad(key_raw.astype(jnp.float32))).astype(jnp.bfloat16)
    value_grad = join(dv_parts).astype(jnp.bfloat16)
    return (normed_out, query_grad, key_grad, value_grad)


def solution(mesh):
    in_specs = (
        P("seq", "head", None),
        P("seq", "head", None),
        P("seq", "head", None),
        P("head", None),
        P("seq", "head", None),
    )
    out_specs = (
        P("seq", "head", None),
        P("seq", "head", None),
        P("seq", "head", None),
        P("seq", "head", None),
    )
    return jax.shard_map(body, mesh=mesh, in_specs=in_specs, out_specs=out_specs, check_vma=False)
```

```python
import jax
import jax.numpy as jnp
from jax import lax
from jax.sharding import PartitionSpec as P

GROUP = 256


def from_behind(shard, axis, by):
    count = lax.axis_size(axis)
    pairs = [(i, i + by) for i in range(count) if 0 <= i + by < count]
    return lax.ppermute(shard, axis, pairs)


def silu_grad(raw):
    sigma = jax.nn.sigmoid(raw)
    return sigma * (1.0 + raw * (1.0 - sigma))


def causal_mask(length):
    rows = lax.broadcasted_iota(jnp.int32, (length, length), 0)
    cols = lax.broadcasted_iota(jnp.int32, (length, length), 1)
    return cols <= rows


def exclusive_scan(own_total, reverse):
    count = lax.axis_size("seq")
    width = own_total.shape[-1]
    rows = own_total.reshape(-1, width)
    size = rows.shape[0]
    chunk = -(-size // count)
    rows = jnp.pad(rows, ((0, chunk * count - size), (0, 0)))
    gathered = lax.all_to_all(rows.reshape(count, chunk, width), "seq", 0, 0, tiled=True)
    inclusive = lax.cumsum(gathered, axis=0, reverse=reverse)
    prefix = inclusive - gathered
    spread = lax.all_to_all(prefix, "seq", 0, 0, tiled=True)
    return spread.reshape(-1, width)[:size].reshape(own_total.shape)


def lower_sum(own_total):
    return exclusive_scan(own_total, False)


def upper_sum(own_total):
    return exclusive_scan(own_total, True)


def mm(lhs, rhs, lhs_dim, rhs_dim):
    dims = (((lhs_dim,), (rhs_dim,)), ((), ()))
    return lax.dot_general(lhs, rhs, dims, preferred_element_type=jnp.float32)


def body(query_raw, key_raw, value_raw, out_gain, out_grad):
    tok_rows, head_count, width = query_raw.shape
    blocks = tok_rows // GROUP
    span = GROUP * head_count
    flat = (tok_rows * head_count, width)
    whole = (tok_rows, head_count, width)
    query_act = jax.nn.silu(query_raw.astype(jnp.float32)).astype(jnp.bfloat16).reshape(flat)
    key_act = jax.nn.silu(key_raw.astype(jnp.float32)).astype(jnp.bfloat16).reshape(flat)
    value_2d = value_raw.reshape(flat)
    row_head = lax.broadcasted_iota(jnp.int32, (span, 1), 0) % head_count
    rows = lax.broadcasted_iota(jnp.int32, (span, span), 0)
    cols = lax.broadcasted_iota(jnp.int32, (span, span), 1)
    mask = (rows % head_count == cols % head_count) & (cols // head_count <= rows // head_count)

    def cut(array, c):
        return array[c * span:(c + 1) * span]

    def per_head(pieces):
        total = jnp.where(row_head == 0, pieces[0], 0.0)
        for h in range(1, head_count):
            total = total + jnp.where(row_head == h, pieces[h], 0.0)
        return total

    def head_outer(lhs, rhs):
        return jnp.stack([mm(jnp.where(row_head == h, lhs, 0), rhs, 0, 0) for h in range(head_count)])

    block_kv = jnp.stack([head_outer(cut(key_act, c), cut(value_2d, c)) for c in range(blocks)])
    own_total = jnp.sum(block_kv, axis=0)
    before = lower_sum(own_total)
    state_b = (before[None] + (jnp.cumsum(block_kv, axis=0) - block_kv)).astype(jnp.bfloat16)
    attn = []
    mixed_rows = []
    for c in range(blocks):
        query_c = cut(query_act, c)
        scores = mm(query_c, cut(key_act, c), 1, 1)
        attn.append(jnp.where(mask, scores, 0.0).astype(jnp.bfloat16))
        local = mm(attn[c], cut(value_2d, c), 1, 0)
        mixed_rows.append(local + per_head([mm(query_c, state_b[c, h], 1, 0) for h in range(head_count)]))
    mixed = jnp.concatenate(mixed_rows, axis=0).reshape(whole)
    grad_in = out_grad.astype(jnp.float32) * out_gain
    sq_part = jnp.sum(mixed * mixed, axis=(1, 2))
    cross_part = jnp.sum(grad_in * mixed, axis=(1, 2))
    both = jnp.stack([sq_part, cross_part])
    both = both + lax.ppermute(both, "head", [(0, 1), (1, 0)])
    sq_total, cross_total = both[0], both[1]
    features = head_count * width * lax.axis_size("head")
    inv_rms = lax.rsqrt(sq_total / features + 1e-06)
    normed_out = (mixed * inv_rms[:, None, None] * out_gain).astype(jnp.bfloat16)
    delta = (
        grad_in * inv_rms[:, None, None]
        - mixed * (cross_total * inv_rms**3 / features)[:, None, None]
    ).astype(jnp.bfloat16)
    delta_2d = delta.reshape(flat)
    block_grad = jnp.stack([head_outer(cut(query_act, c), cut(delta_2d, c)) for c in range(blocks)])
    own_grad = jnp.sum(block_grad, axis=0)
    after = upper_sum(own_grad)
    local_after = lax.cumsum(block_grad, axis=0, reverse=True) - block_grad
    grad_state = (after[None] + local_after).astype(jnp.bfloat16)
    dq_rows, dk_rows, dv_rows = [], [], []
    for c in range(blocks):
        query_c, key_c, value_c, delta_c = (cut(a, c) for a in (query_act, key_act, value_2d, delta_2d))
        bscore = jnp.where(mask, mm(delta_c, value_c, 1, 1), 0.0).astype(jnp.bfloat16)
        dq_rows.append(mm(bscore, key_c, 1, 0) + per_head([mm(delta_c, state_b[c, h], 1, 1) for h in range(head_count)]))
        dk_rows.append(mm(bscore, query_c, 0, 0) + per_head([mm(value_c, grad_state[c, h], 1, 1) for h in range(head_count)]))
        dv_rows.append(mm(attn[c], delta_c, 0, 0) + per_head([mm(key_c, grad_state[c, h], 1, 0) for h in range(head_count)]))
    dquery = jnp.concatenate(dq_rows, axis=0).reshape(whole)
    dkey = jnp.concatenate(dk_rows, axis=0).reshape(whole)
    dvalue = jnp.concatenate(dv_rows, axis=0).reshape(whole)
    query_grad = (dquery * silu_grad(query_raw.astype(jnp.float32))).astype(jnp.bfloat16)
    key_grad = (dkey * silu_grad(key_raw.astype(jnp.float32))).astype(jnp.bfloat16)
    value_grad = dvalue.astype(jnp.bfloat16)
    return (normed_out, query_grad, key_grad, value_grad)


def solution(mesh):
    in_specs = (
        P("seq", "head", None),
        P("seq", "head", None),
        P("seq", "head", None),
        P("head", None),
        P("seq", "head", None),
    )
    out_specs = (
        P("seq", "head", None),
        P("seq", "head", None),
        P("seq", "head", None),
        P("seq", "head", None),
    )
    return jax.shard_map(body, mesh=mesh, in_specs=in_specs, out_specs=out_specs, check_vma=False)
```

```python
import jax
import jax.numpy as jnp
from jax import lax
from jax.sharding import PartitionSpec as P

GROUP = 256


def from_behind(shard, axis, by):
    count = lax.axis_size(axis)
    pairs = [(i, i + by) for i in range(count) if 0 <= i + by < count]
    return lax.ppermute(shard, axis, pairs)


def silu_grad(raw):
    sigma = jax.nn.sigmoid(raw)
    return sigma * (1.0 + raw * (1.0 - sigma))


def causal_mask(length):
    rows = lax.broadcasted_iota(jnp.int32, (length, length), 0)
    cols = lax.broadcasted_iota(jnp.int32, (length, length), 1)
    return cols <= rows


def exclusive_scan(own_total, reverse):
    count = lax.axis_size("seq")
    width = own_total.shape[-1]
    rows = own_total.reshape(-1, width)
    size = rows.shape[0]
    chunk = -(-size // count)
    rows = jnp.pad(rows, ((0, chunk * count - size), (0, 0)))
    gathered = lax.all_to_all(rows.reshape(count, chunk, width), "seq", 0, 0, tiled=True)
    inclusive = lax.cumsum(gathered, axis=0, reverse=reverse)
    prefix = inclusive - gathered
    spread = lax.all_to_all(prefix, "seq", 0, 0, tiled=True)
    return spread.reshape(-1, width)[:size].reshape(own_total.shape)


def lower_sum(own_total):
    return exclusive_scan(own_total, False)


def upper_sum(own_total):
    return exclusive_scan(own_total, True)


def body(query_raw, key_raw, value_raw, out_gain, out_grad):
    tok_rows, head_count, width = query_raw.shape
    blocks = tok_rows // GROUP
    blocked = (blocks, GROUP, head_count, width)
    query_act = jax.nn.silu(query_raw.astype(jnp.float32)).astype(jnp.bfloat16).reshape(blocked)
    key_act = jax.nn.silu(key_raw.astype(jnp.float32)).astype(jnp.bfloat16).reshape(blocked)
    value_blk = value_raw.reshape(blocked)
    mask = causal_mask(GROUP)[None, None]
    block_kv = jnp.einsum("cshd,cshe->chde", key_act, value_blk, preferred_element_type=jnp.float32)
    own_total = jnp.sum(block_kv, axis=0)
    before = lower_sum(own_total)
    if blocks == 1:
        state_b = before[None]
    else:
        state_b = before[None] + (jnp.cumsum(block_kv, axis=0) - block_kv)
    scores = jnp.einsum("cthd,cshd->chts", query_act, key_act, preferred_element_type=jnp.float32)
    attn = jnp.where(mask, scores, 0.0).astype(jnp.bfloat16)
    mixed = jnp.einsum("chts,cshe->cthe", attn, value_blk, preferred_element_type=jnp.float32)
    mixed = mixed + jnp.einsum(
        "cthd,chde->cthe", query_act, state_b, preferred_element_type=jnp.float32, precision=lax.Precision.HIGHEST
    )
    mixed = mixed.reshape(tok_rows, head_count, width)
    grad_in = out_grad.astype(jnp.float32) * out_gain
    sq_part = jnp.sum(mixed * mixed, axis=(1, 2))
    cross_part = jnp.sum(grad_in * mixed, axis=(1, 2))
    both = jnp.stack([sq_part, cross_part])
    both = both + lax.ppermute(both, "head", [(0, 1), (1, 0)])
    sq_total, cross_total = both[0], both[1]
    features = head_count * width * lax.axis_size("head")
    inv_rms = lax.rsqrt(sq_total / features + 1e-06)
    normed_out = (mixed * inv_rms[:, None, None] * out_gain).astype(jnp.bfloat16)
    delta = (
        grad_in * inv_rms[:, None, None]
        - mixed * (cross_total * inv_rms**3 / features)[:, None, None]
    ).astype(jnp.bfloat16)
    delta_blk = delta.reshape(blocked)
    block_grad = jnp.einsum(
        "cthd,cthe->chde", query_act, delta_blk, preferred_element_type=jnp.float32
    )
    own_grad = jnp.sum(block_grad, axis=0)
    after = upper_sum(own_grad)
    if blocks == 1:
        grad_state = after[None]
    else:
        grad_state = after[None] + (lax.cumsum(block_grad, axis=0, reverse=True) - block_grad)
    bscore = jnp.einsum("cthe,cshe->chts", delta_blk, value_blk, preferred_element_type=jnp.float32)
    bscore = jnp.where(mask, bscore, 0.0).astype(jnp.bfloat16)
    dquery = jnp.einsum("chts,cshd->cthd", bscore, key_act, preferred_element_type=jnp.float32)
    dquery = dquery + jnp.einsum(
        "cthe,chde->cthd", delta_blk, state_b, preferred_element_type=jnp.float32, precision=lax.Precision.HIGHEST
    )
    dkey = jnp.einsum("chts,cthd->cshd", bscore, query_act, preferred_element_type=jnp.float32)
    dkey = dkey + jnp.einsum(
        "cshe,chde->cshd", value_blk, grad_state, preferred_element_type=jnp.float32, precision=lax.Precision.HIGHEST
    )
    dvalue = jnp.einsum("chts,cthe->cshe", attn, delta_blk, preferred_element_type=jnp.float32)
    dvalue = dvalue + jnp.einsum(
        "cshd,chde->cshe", key_act, grad_state, preferred_element_type=jnp.float32, precision=lax.Precision.HIGHEST
    )
    whole = (tok_rows, head_count, width)
    query_grad = (dquery.reshape(whole) * silu_grad(query_raw.astype(jnp.float32))).astype(
        jnp.bfloat16
    )
    key_grad = (dkey.reshape(whole) * silu_grad(key_raw.astype(jnp.float32))).astype(jnp.bfloat16)
    value_grad = dvalue.reshape(whole).astype(jnp.bfloat16)
    return (normed_out, query_grad, key_grad, value_grad)


def solution(mesh):
    in_specs = (
        P("seq", "head", None),
        P("seq", "head", None),
        P("seq", "head", None),
        P("head", None),
        P("seq", "head", None),
    )
    out_specs = (
        P("seq", "head", None),
        P("seq", "head", None),
        P("seq", "head", None),
        P("seq", "head", None),
    )
    return jax.shard_map(body, mesh=mesh, in_specs=in_specs, out_specs=out_specs, check_vma=False)
```

```python
import jax
import jax.numpy as jnp
from jax import lax
from jax.sharding import PartitionSpec as P
from jax.experimental import pallas as pl

GROUP = 256


def from_behind(shard, axis, by):
    count = lax.axis_size(axis)
    pairs = [(i, i + by) for i in range(count) if 0 <= i + by < count]
    return lax.ppermute(shard, axis, pairs)


def silu_grad(raw):
    sigma = jax.nn.sigmoid(raw)
    return sigma * (1.0 + raw * (1.0 - sigma))


def causal_mask(length):
    rows = lax.broadcasted_iota(jnp.int32, (length, length), 0)
    cols = lax.broadcasted_iota(jnp.int32, (length, length), 1)
    return cols <= rows


def exclusive_scan(own_total, reverse):
    count = lax.axis_size("seq")
    width = own_total.shape[-1]
    rows = own_total.reshape(-1, width)
    size = rows.shape[0]
    chunk = -(-size // count)
    rows = jnp.pad(rows, ((0, chunk * count - size), (0, 0)))
    gathered = lax.all_to_all(rows.reshape(count, chunk, width), "seq", 0, 0, tiled=True)
    inclusive = lax.cumsum(gathered, axis=0, reverse=reverse)
    prefix = inclusive - gathered
    spread = lax.all_to_all(prefix, "seq", 0, 0, tiled=True)
    return spread.reshape(-1, width)[:size].reshape(own_total.shape)


def lower_sum(own_total):
    return exclusive_scan(own_total, False)


def upper_sum(own_total):
    return exclusive_scan(own_total, True)


def head_outer(lhs_rows, rhs_rows, head_count, lhs_silu):
    span = GROUP * head_count
    width = lhs_rows.shape[-1]
    blocks = lhs_rows.shape[0] // span

    def kernel(lhs_ref, rhs_ref, out_ref):
        lhs = lhs_ref[...]
        if lhs_silu:
            lhs = jax.nn.silu(lhs.astype(jnp.float32)).astype(jnp.bfloat16)
        rhs = rhs_ref[...]
        row_head = lax.broadcasted_iota(jnp.int32, lhs.shape, 0) % head_count
        for h in range(head_count):
            picked = jnp.where(row_head == h, lhs, jnp.zeros_like(lhs))
            out_ref[h] = lax.dot_general(
                picked, rhs, (((0,), (0,)), ((), ())), preferred_element_type=jnp.float32
            )

    return pl.pallas_call(
        kernel,
        grid=(blocks,),
        in_specs=[
            pl.BlockSpec((span, width), lambda c: (c, 0)),
            pl.BlockSpec((span, width), lambda c: (c, 0)),
        ],
        out_specs=pl.BlockSpec((None, head_count, width, width), lambda c: (c, 0, 0, 0)),
        out_shape=jax.ShapeDtypeStruct((blocks, head_count, width, width), jnp.float32),
    )(lhs_rows, rhs_rows)


def body(query_raw, key_raw, value_raw, out_gain, out_grad):
    tok_rows, head_count, width = query_raw.shape
    blocks = tok_rows // GROUP
    blocked = (blocks, GROUP, head_count, width)
    query_act = jax.nn.silu(query_raw.astype(jnp.float32)).astype(jnp.bfloat16).reshape(blocked)
    key_act = jax.nn.silu(key_raw.astype(jnp.float32)).astype(jnp.bfloat16).reshape(blocked)
    value_blk = value_raw.reshape(blocked)
    mask = causal_mask(GROUP)[None, None]
    rows = (tok_rows * head_count, width)
    block_kv = head_outer(key_raw.reshape(rows), value_raw.reshape(rows), head_count, True)
    own_total = jnp.sum(block_kv, axis=0)
    before = lower_sum(own_total)
    if blocks == 1:
        state_b = before[None]
    else:
        state_b = before[None] + (jnp.cumsum(block_kv, axis=0) - block_kv)
    scores = jnp.einsum("cthd,cshd->chts", query_act, key_act, preferred_element_type=jnp.float32)
    attn = jnp.where(mask, scores, 0.0).astype(jnp.bfloat16)
    mixed = jnp.einsum("chts,cshe->cthe", attn, value_blk, preferred_element_type=jnp.float32)
    mixed = mixed + jnp.einsum(
        "cthd,chde->cthe", query_act, state_b, preferred_element_type=jnp.float32, precision=lax.Precision.HIGHEST
    )
    mixed = mixed.reshape(tok_rows, head_count, width)
    grad_in = out_grad.astype(jnp.float32) * out_gain
    sq_part = jnp.sum(mixed * mixed, axis=(1, 2))
    cross_part = jnp.sum(grad_in * mixed, axis=(1, 2))
    both = jnp.stack([sq_part, cross_part])
    both = both + lax.ppermute(both, "head", [(0, 1), (1, 0)])
    sq_total, cross_total = both[0], both[1]
    features = head_count * width * lax.axis_size("head")
    inv_rms = lax.rsqrt(sq_total / features + 1e-06)
    normed_out = (mixed * inv_rms[:, None, None] * out_gain).astype(jnp.bfloat16)
    delta = (
        grad_in * inv_rms[:, None, None]
        - mixed * (cross_total * inv_rms**3 / features)[:, None, None]
    ).astype(jnp.bfloat16)
    delta_blk = delta.reshape(blocked)
    block_grad = head_outer(query_raw.reshape(rows), delta.reshape(rows), head_count, True)
    own_grad = jnp.sum(block_grad, axis=0)
    after = upper_sum(own_grad)
    if blocks == 1:
        grad_state = after[None]
    else:
        grad_state = after[None] + (lax.cumsum(block_grad, axis=0, reverse=True) - block_grad)
    bscore = jnp.einsum("cthe,cshe->chts", delta_blk, value_blk, preferred_element_type=jnp.float32)
    bscore = jnp.where(mask, bscore, 0.0).astype(jnp.bfloat16)
    dquery = jnp.einsum("chts,cshd->cthd", bscore, key_act, preferred_element_type=jnp.float32)
    dquery = dquery + jnp.einsum(
        "cthe,chde->cthd", delta_blk, state_b, preferred_element_type=jnp.float32, precision=lax.Precision.HIGHEST
    )
    dkey = jnp.einsum("chts,cthd->cshd", bscore, query_act, preferred_element_type=jnp.float32)
    dkey = dkey + jnp.einsum(
        "cshe,chde->cshd", value_blk, grad_state, preferred_element_type=jnp.float32, precision=lax.Precision.HIGHEST
    )
    dvalue = jnp.einsum("chts,cthe->cshe", attn, delta_blk, preferred_element_type=jnp.float32)
    dvalue = dvalue + jnp.einsum(
        "cshd,chde->cshe", key_act, grad_state, preferred_element_type=jnp.float32, precision=lax.Precision.HIGHEST
    )
    whole = (tok_rows, head_count, width)
    query_grad = (dquery.reshape(whole) * silu_grad(query_raw.astype(jnp.float32))).astype(
        jnp.bfloat16
    )
    key_grad = (dkey.reshape(whole) * silu_grad(key_raw.astype(jnp.float32))).astype(jnp.bfloat16)
    value_grad = dvalue.reshape(whole).astype(jnp.bfloat16)
    return (normed_out, query_grad, key_grad, value_grad)


def solution(mesh):
    in_specs = (
        P("seq", "head", None),
        P("seq", "head", None),
        P("seq", "head", None),
        P("head", None),
        P("seq", "head", None),
    )
    out_specs = (
        P("seq", "head", None),
        P("seq", "head", None),
        P("seq", "head", None),
        P("seq", "head", None),
    )
    return jax.shard_map(body, mesh=mesh, in_specs=in_specs, out_specs=out_specs, check_vma=False)
```

```python
import jax
import jax.numpy as jnp
from jax import lax
from jax.sharding import PartitionSpec as P
from jax.experimental import pallas as pl

GROUP = 256


def from_behind(shard, axis, by):
    count = lax.axis_size(axis)
    pairs = [(i, i + by) for i in range(count) if 0 <= i + by < count]
    return lax.ppermute(shard, axis, pairs)


def silu_grad(raw):
    sigma = jax.nn.sigmoid(raw)
    return sigma * (1.0 + raw * (1.0 - sigma))


def causal_mask(length):
    rows = lax.broadcasted_iota(jnp.int32, (length, length), 0)
    cols = lax.broadcasted_iota(jnp.int32, (length, length), 1)
    return cols <= rows


def exclusive_scan(own_total, reverse):
    count = lax.axis_size("seq")
    width = own_total.shape[-1]
    rows = own_total.reshape(-1, width)
    size = rows.shape[0]
    chunk = -(-size // count)
    rows = jnp.pad(rows, ((0, chunk * count - size), (0, 0)))
    gathered = lax.all_to_all(rows.reshape(count, chunk, width), "seq", 0, 0, tiled=True)
    inclusive = lax.cumsum(gathered, axis=0, reverse=reverse)
    prefix = inclusive - gathered
    spread = lax.all_to_all(prefix, "seq", 0, 0, tiled=True)
    return spread.reshape(-1, width)[:size].reshape(own_total.shape)


def lower_sum(own_total):
    return exclusive_scan(own_total, False)


def upper_sum(own_total):
    return exclusive_scan(own_total, True)


def head_outer(lhs_rows, rhs_rows, head_count, lhs_silu):
    span = GROUP * head_count
    width = lhs_rows.shape[-1]
    blocks = lhs_rows.shape[0] // span

    def kernel(lhs_ref, rhs_ref, out_ref):
        lhs = lhs_ref[...]
        if lhs_silu:
            lhs = jax.nn.silu(lhs.astype(jnp.float32)).astype(jnp.bfloat16)
        rhs = rhs_ref[...]
        lhs_t = lhs.T
        col_head = lax.broadcasted_iota(jnp.int32, lhs_t.shape, 1) % head_count
        for h in range(head_count):
            picked = jnp.where(col_head == h, lhs_t, jnp.zeros_like(lhs_t))
            out_ref[h] = jnp.dot(picked, rhs, preferred_element_type=jnp.float32)

    return pl.pallas_call(
        kernel,
        grid=(blocks,),
        in_specs=[
            pl.BlockSpec((span, width), lambda c: (c, 0)),
            pl.BlockSpec((span, width), lambda c: (c, 0)),
        ],
        out_specs=pl.BlockSpec((None, head_count, width, width), lambda c: (c, 0, 0, 0)),
        out_shape=jax.ShapeDtypeStruct((blocks, head_count, width, width), jnp.float32),
    )(lhs_rows, rhs_rows)


def body(query_raw, key_raw, value_raw, out_gain, out_grad):
    tok_rows, head_count, width = query_raw.shape
    blocks = tok_rows // GROUP
    blocked = (blocks, GROUP, head_count, width)
    query_act = jax.nn.silu(query_raw.astype(jnp.float32)).astype(jnp.bfloat16).reshape(blocked)
    key_act = jax.nn.silu(key_raw.astype(jnp.float32)).astype(jnp.bfloat16).reshape(blocked)
    value_blk = value_raw.reshape(blocked)
    mask = causal_mask(GROUP)[None, None]
    rows = (tok_rows * head_count, width)
    block_kv = head_outer(key_raw.reshape(rows), value_raw.reshape(rows), head_count, True)
    own_total = jnp.sum(block_kv, axis=0)
    before = lower_sum(own_total)
    if blocks == 1:
        state_b = before[None]
    else:
        state_b = before[None] + (jnp.cumsum(block_kv, axis=0) - block_kv)
    scores = jnp.einsum("cthd,cshd->chts", query_act, key_act, preferred_element_type=jnp.float32)
    attn = jnp.where(mask, scores, 0.0).astype(jnp.bfloat16)
    mixed = jnp.einsum("chts,cshe->cthe", attn, value_blk, preferred_element_type=jnp.float32)
    mixed = mixed + jnp.einsum(
        "cthd,chde->cthe", query_act, state_b, preferred_element_type=jnp.float32, precision=lax.Precision.HIGHEST
    )
    mixed = mixed.reshape(tok_rows, head_count, width)
    grad_in = out_grad.astype(jnp.float32) * out_gain
    sq_part = jnp.sum(mixed * mixed, axis=(1, 2))
    cross_part = jnp.sum(grad_in * mixed, axis=(1, 2))
    both = jnp.stack([sq_part, cross_part])
    both = both + lax.ppermute(both, "head", [(0, 1), (1, 0)])
    sq_total, cross_total = both[0], both[1]
    features = head_count * width * lax.axis_size("head")
    inv_rms = lax.rsqrt(sq_total / features + 1e-06)
    normed_out = (mixed * inv_rms[:, None, None] * out_gain).astype(jnp.bfloat16)
    delta = (
        grad_in * inv_rms[:, None, None]
        - mixed * (cross_total * inv_rms**3 / features)[:, None, None]
    ).astype(jnp.bfloat16)
    delta_blk = delta.reshape(blocked)
    block_grad = jnp.einsum(
        "cthd,cthe->chde", query_act, delta_blk, preferred_element_type=jnp.float32
    )
    own_grad = jnp.sum(block_grad, axis=0)
    after = upper_sum(own_grad)
    if blocks == 1:
        grad_state = after[None]
    else:
        grad_state = after[None] + (lax.cumsum(block_grad, axis=0, reverse=True) - block_grad)
    bscore = jnp.einsum("cthe,cshe->chts", delta_blk, value_blk, preferred_element_type=jnp.float32)
    bscore = jnp.where(mask, bscore, 0.0).astype(jnp.bfloat16)
    dquery = jnp.einsum("chts,cshd->cthd", bscore, key_act, preferred_element_type=jnp.float32)
    dquery = dquery + jnp.einsum(
        "cthe,chde->cthd", delta_blk, state_b, preferred_element_type=jnp.float32, precision=lax.Precision.HIGHEST
    )
    dkey = jnp.einsum("chts,cthd->cshd", bscore, query_act, preferred_element_type=jnp.float32)
    dkey = dkey + jnp.einsum(
        "cshe,chde->cshd", value_blk, grad_state, preferred_element_type=jnp.float32, precision=lax.Precision.HIGHEST
    )
    dvalue = jnp.einsum("chts,cthe->cshe", attn, delta_blk, preferred_element_type=jnp.float32)
    dvalue = dvalue + jnp.einsum(
        "cshd,chde->cshe", key_act, grad_state, preferred_element_type=jnp.float32, precision=lax.Precision.HIGHEST
    )
    whole = (tok_rows, head_count, width)
    query_grad = (dquery.reshape(whole) * silu_grad(query_raw.astype(jnp.float32))).astype(
        jnp.bfloat16
    )
    key_grad = (dkey.reshape(whole) * silu_grad(key_raw.astype(jnp.float32))).astype(jnp.bfloat16)
    value_grad = dvalue.reshape(whole).astype(jnp.bfloat16)
    return (normed_out, query_grad, key_grad, value_grad)


def solution(mesh):
    in_specs = (
        P("seq", "head", None),
        P("seq", "head", None),
        P("seq", "head", None),
        P("head", None),
        P("seq", "head", None),
    )
    out_specs = (
        P("seq", "head", None),
        P("seq", "head", None),
        P("seq", "head", None),
        P("seq", "head", None),
    )
    return jax.shard_map(body, mesh=mesh, in_specs=in_specs, out_specs=out_specs, check_vma=False)
```

```python
import jax
import jax.numpy as jnp
from jax import lax
from jax.sharding import PartitionSpec as P
from jax.experimental.layout import Layout, with_layout_constraint

GROUP = 256


def from_behind(shard, axis, by):
    count = lax.axis_size(axis)
    pairs = [(i, i + by) for i in range(count) if 0 <= i + by < count]
    return lax.ppermute(shard, axis, pairs)


def silu_grad(raw):
    sigma = jax.nn.sigmoid(raw)
    return sigma * (1.0 + raw * (1.0 - sigma))


def causal_mask(length):
    rows = lax.broadcasted_iota(jnp.int32, (length, length), 0)
    cols = lax.broadcasted_iota(jnp.int32, (length, length), 1)
    return cols <= rows


def exclusive_scan(own_total, reverse):
    count = lax.axis_size("seq")
    width = own_total.shape[-1]
    rows = own_total.reshape(-1, width)
    size = rows.shape[0]
    chunk = -(-size // count)
    rows = jnp.pad(rows, ((0, chunk * count - size), (0, 0)))
    gathered = lax.all_to_all(rows.reshape(count, chunk, width), "seq", 0, 0, tiled=True)
    inclusive = lax.cumsum(gathered, axis=0, reverse=reverse)
    prefix = inclusive - gathered
    spread = lax.all_to_all(prefix, "seq", 0, 0, tiled=True)
    return spread.reshape(-1, width)[:size].reshape(own_total.shape)


def lower_sum(own_total):
    return exclusive_scan(own_total, False)


def upper_sum(own_total):
    return exclusive_scan(own_total, True)


def natural(array):
    return with_layout_constraint(array, Layout(tuple(range(array.ndim))))


def body(query_raw, key_raw, value_raw, out_gain, out_grad):
    tok_rows, head_count, width = query_raw.shape
    blocks = tok_rows // GROUP
    blocked = (blocks, GROUP, head_count, width)
    query_act = jax.nn.silu(query_raw.astype(jnp.float32)).astype(jnp.bfloat16).reshape(blocked)
    key_act = jax.nn.silu(key_raw.astype(jnp.float32)).astype(jnp.bfloat16).reshape(blocked)
    value_blk = value_raw.reshape(blocked)
    mask = causal_mask(GROUP)[None, None]
    block_kv = jnp.einsum("cshd,cshe->chde", key_act, value_blk, preferred_element_type=jnp.float32)
    own_total = jnp.sum(block_kv, axis=0)
    before = lower_sum(own_total)
    if blocks == 1:
        state_b = before[None]
    else:
        state_b = before[None] + (jnp.cumsum(block_kv, axis=0) - block_kv)
    scores = jnp.einsum("cthd,cshd->chts", query_act, key_act, preferred_element_type=jnp.float32)
    attn = jnp.where(mask, scores, 0.0).astype(jnp.bfloat16)
    mixed = jnp.einsum("chts,cshe->cthe", attn, value_blk, preferred_element_type=jnp.float32)
    mixed = mixed + jnp.einsum(
        "cthd,chde->cthe", query_act, state_b, preferred_element_type=jnp.float32, precision=lax.Precision.HIGHEST
    )
    mixed = natural(mixed.reshape(tok_rows, head_count, width))
    grad_in = out_grad.astype(jnp.float32) * out_gain
    sq_part = jnp.sum(mixed * mixed, axis=(1, 2))
    cross_part = jnp.sum(grad_in * mixed, axis=(1, 2))
    both = jnp.stack([sq_part, cross_part])
    both = both + lax.ppermute(both, "head", [(0, 1), (1, 0)])
    sq_total, cross_total = both[0], both[1]
    features = head_count * width * lax.axis_size("head")
    inv_rms = lax.rsqrt(sq_total / features + 1e-06)
    normed_out = (mixed * inv_rms[:, None, None] * out_gain).astype(jnp.bfloat16)
    delta = (
        grad_in * inv_rms[:, None, None]
        - mixed * (cross_total * inv_rms**3 / features)[:, None, None]
    ).astype(jnp.bfloat16)
    delta_blk = delta.reshape(blocked)
    block_grad = jnp.einsum(
        "cthd,cthe->chde", query_act, delta_blk, preferred_element_type=jnp.float32
    )
    own_grad = jnp.sum(block_grad, axis=0)
    after = upper_sum(own_grad)
    if blocks == 1:
        grad_state = after[None]
    else:
        grad_state = after[None] + (lax.cumsum(block_grad, axis=0, reverse=True) - block_grad)
    bscore = jnp.einsum("cthe,cshe->chts", delta_blk, value_blk, preferred_element_type=jnp.float32)
    bscore = jnp.where(mask, bscore, 0.0).astype(jnp.bfloat16)
    dquery = jnp.einsum("chts,cshd->cthd", bscore, key_act, preferred_element_type=jnp.float32)
    dquery = dquery + jnp.einsum(
        "cthe,chde->cthd", delta_blk, state_b, preferred_element_type=jnp.float32, precision=lax.Precision.HIGHEST
    )
    dkey = jnp.einsum("chts,cthd->cshd", bscore, query_act, preferred_element_type=jnp.float32)
    dkey = dkey + jnp.einsum(
        "cshe,chde->cshd", value_blk, grad_state, preferred_element_type=jnp.float32, precision=lax.Precision.HIGHEST
    )
    dvalue = jnp.einsum("chts,cthe->cshe", attn, delta_blk, preferred_element_type=jnp.float32)
    dvalue = dvalue + jnp.einsum(
        "cshd,chde->cshe", key_act, grad_state, preferred_element_type=jnp.float32, precision=lax.Precision.HIGHEST
    )
    whole = (tok_rows, head_count, width)
    dquery, dkey, dvalue = natural(dquery), natural(dkey), natural(dvalue)
    query_grad = (dquery.reshape(whole) * silu_grad(query_raw.astype(jnp.float32))).astype(
        jnp.bfloat16
    )
    key_grad = (dkey.reshape(whole) * silu_grad(key_raw.astype(jnp.float32))).astype(jnp.bfloat16)
    value_grad = dvalue.reshape(whole).astype(jnp.bfloat16)
    return (normed_out, query_grad, key_grad, value_grad)


def solution(mesh):
    in_specs = (
        P("seq", "head", None),
        P("seq", "head", None),
        P("seq", "head", None),
        P("head", None),
        P("seq", "head", None),
    )
    out_specs = (
        P("seq", "head", None),
        P("seq", "head", None),
        P("seq", "head", None),
        P("seq", "head", None),
    )
    return jax.shard_map(body, mesh=mesh, in_specs=in_specs, out_specs=out_specs, check_vma=False)
```

```python
import jax
import jax.numpy as jnp
from jax import lax
from jax.sharding import PartitionSpec as P
from jax.experimental import pallas as pl

GROUP = 256


def from_behind(shard, axis, by):
    count = lax.axis_size(axis)
    pairs = [(i, i + by) for i in range(count) if 0 <= i + by < count]
    return lax.ppermute(shard, axis, pairs)


def silu_grad(raw):
    sigma = jax.nn.sigmoid(raw)
    return sigma * (1.0 + raw * (1.0 - sigma))


def causal_mask(length):
    rows = lax.broadcasted_iota(jnp.int32, (length, length), 0)
    cols = lax.broadcasted_iota(jnp.int32, (length, length), 1)
    return cols <= rows


def exclusive_scan(own_total, reverse):
    count = lax.axis_size("seq")
    width = own_total.shape[-1]
    rows = own_total.reshape(-1, width)
    size = rows.shape[0]
    chunk = -(-size // count)
    rows = jnp.pad(rows, ((0, chunk * count - size), (0, 0)))
    gathered = lax.all_to_all(rows.reshape(count, chunk, width), "seq", 0, 0, tiled=True)
    inclusive = lax.cumsum(gathered, axis=0, reverse=reverse)
    prefix = inclusive - gathered
    spread = lax.all_to_all(prefix, "seq", 0, 0, tiled=True)
    return spread.reshape(-1, width)[:size].reshape(own_total.shape)


def lower_sum(own_total):
    return exclusive_scan(own_total, False)


def upper_sum(own_total):
    return exclusive_scan(own_total, True)


def mm(lhs, rhs, lhs_dim, rhs_dim):
    dims = (((lhs_dim,), (rhs_dim,)), ((), ()))
    return lax.dot_general(lhs, rhs, dims, preferred_element_type=jnp.float32)


def backward_tail(query_raw, key_raw, value_raw, delta, bscore, attn, state, grad_state):
    tok_rows, head_count, width = query_raw.shape
    blocks = tok_rows // GROUP

    def kernel(qr_ref, kr_ref, v_ref, d_ref, bs_ref, at_ref, st_ref, gs_ref, qg_ref, kg_ref, vg_ref):
        for h in range(head_count):
            q_raw = qr_ref[:, h, :].astype(jnp.float32)
            k_raw = kr_ref[:, h, :].astype(jnp.float32)
            q_act = jax.nn.silu(q_raw).astype(jnp.bfloat16)
            k_act = jax.nn.silu(k_raw).astype(jnp.bfloat16)
            value = v_ref[:, h, :]
            delta_h = d_ref[:, h, :]
            bs = bs_ref[h]
            at = at_ref[h]
            state_b = st_ref[h].astype(jnp.bfloat16)
            grad_b = gs_ref[h].astype(jnp.bfloat16)
            dq = mm(bs, k_act, 1, 0) + mm(delta_h, state_b, 1, 1)
            dk = mm(bs, q_act, 0, 0) + mm(value, grad_b, 1, 1)
            dv = mm(at, delta_h, 0, 0) + mm(k_act, grad_b, 1, 0)
            qg_ref[:, h, :] = (dq * silu_grad(q_raw)).astype(jnp.bfloat16)
            kg_ref[:, h, :] = (dk * silu_grad(k_raw)).astype(jnp.bfloat16)
            vg_ref[:, h, :] = dv.astype(jnp.bfloat16)

    rows = pl.BlockSpec((GROUP, head_count, width), lambda c: (c, 0, 0))
    square = pl.BlockSpec((None, head_count, GROUP, GROUP), lambda c: (c, 0, 0, 0))
    states = pl.BlockSpec((None, head_count, width, width), lambda c: (c, 0, 0, 0))
    out = jax.ShapeDtypeStruct(query_raw.shape, jnp.bfloat16)
    return pl.pallas_call(
        kernel,
        grid=(blocks,),
        in_specs=[rows, rows, rows, rows, square, square, states, states],
        out_specs=[rows, rows, rows],
        out_shape=[out, out, out],
    )(query_raw, key_raw, value_raw, delta, bscore, attn, state, grad_state)


def body(query_raw, key_raw, value_raw, out_gain, out_grad):
    tok_rows, head_count, width = query_raw.shape
    blocks = tok_rows // GROUP
    blocked = (blocks, GROUP, head_count, width)
    query_act = jax.nn.silu(query_raw.astype(jnp.float32)).astype(jnp.bfloat16).reshape(blocked)
    key_act = jax.nn.silu(key_raw.astype(jnp.float32)).astype(jnp.bfloat16).reshape(blocked)
    value_blk = value_raw.reshape(blocked)
    mask = causal_mask(GROUP)[None, None]
    block_kv = jnp.einsum("cshd,cshe->chde", key_act, value_blk, preferred_element_type=jnp.float32)
    own_total = jnp.sum(block_kv, axis=0)
    before = lower_sum(own_total)
    if blocks == 1:
        state_b = before[None]
    else:
        state_b = before[None] + (jnp.cumsum(block_kv, axis=0) - block_kv)
    scores = jnp.einsum("cthd,cshd->chts", query_act, key_act, preferred_element_type=jnp.float32)
    attn = jnp.where(mask, scores, 0.0).astype(jnp.bfloat16)
    mixed = jnp.einsum("chts,cshe->cthe", attn, value_blk, preferred_element_type=jnp.float32)
    mixed = mixed + jnp.einsum(
        "cthd,chde->cthe", query_act, state_b, preferred_element_type=jnp.float32, precision=lax.Precision.HIGHEST
    )
    mixed = mixed.reshape(tok_rows, head_count, width)
    grad_in = out_grad.astype(jnp.float32) * out_gain
    sq_part = jnp.sum(mixed * mixed, axis=(1, 2))
    cross_part = jnp.sum(grad_in * mixed, axis=(1, 2))
    both = jnp.stack([sq_part, cross_part])
    both = both + lax.ppermute(both, "head", [(0, 1), (1, 0)])
    sq_total, cross_total = both[0], both[1]
    features = head_count * width * lax.axis_size("head")
    inv_rms = lax.rsqrt(sq_total / features + 1e-06)
    normed_out = (mixed * inv_rms[:, None, None] * out_gain).astype(jnp.bfloat16)
    delta = (
        grad_in * inv_rms[:, None, None]
        - mixed * (cross_total * inv_rms**3 / features)[:, None, None]
    ).astype(jnp.bfloat16)
    delta_blk = delta.reshape(blocked)
    block_grad = jnp.einsum(
        "cthd,cthe->chde", query_act, delta_blk, preferred_element_type=jnp.float32
    )
    own_grad = jnp.sum(block_grad, axis=0)
    after = upper_sum(own_grad)
    if blocks == 1:
        grad_state = after[None]
    else:
        grad_state = after[None] + (lax.cumsum(block_grad, axis=0, reverse=True) - block_grad)
    bscore = jnp.einsum("cthe,cshe->chts", delta_blk, value_blk, preferred_element_type=jnp.float32)
    bscore = jnp.where(mask, bscore, 0.0).astype(jnp.bfloat16)
    query_grad, key_grad, value_grad = backward_tail(
        query_raw, key_raw, value_raw, delta, bscore, attn, state_b, grad_state
    )
    return (normed_out, query_grad, key_grad, value_grad)


def solution(mesh):
    in_specs = (
        P("seq", "head", None),
        P("seq", "head", None),
        P("seq", "head", None),
        P("head", None),
        P("seq", "head", None),
    )
    out_specs = (
        P("seq", "head", None),
        P("seq", "head", None),
        P("seq", "head", None),
        P("seq", "head", None),
    )
    return jax.shard_map(body, mesh=mesh, in_specs=in_specs, out_specs=out_specs, check_vma=False)
```

```python
import jax
import jax.numpy as jnp
from jax import lax
from jax.sharding import PartitionSpec as P
from jax.experimental.layout import Layout, with_layout_constraint

GROUP = 256


def from_behind(shard, axis, by):
    count = lax.axis_size(axis)
    pairs = [(i, i + by) for i in range(count) if 0 <= i + by < count]
    return lax.ppermute(shard, axis, pairs)


def silu_grad(raw):
    sigma = jax.nn.sigmoid(raw)
    return sigma * (1.0 + raw * (1.0 - sigma))


def causal_mask(length):
    rows = lax.broadcasted_iota(jnp.int32, (length, length), 0)
    cols = lax.broadcasted_iota(jnp.int32, (length, length), 1)
    return cols <= rows


def exclusive_scan(own_total, reverse):
    count = lax.axis_size("seq")
    width = own_total.shape[-1]
    rows = own_total.reshape(-1, width)
    size = rows.shape[0]
    chunk = -(-size // count)
    rows = jnp.pad(rows, ((0, chunk * count - size), (0, 0)))
    gathered = lax.all_to_all(rows.reshape(count, chunk, width), "seq", 0, 0, tiled=True)
    inclusive = lax.cumsum(gathered, axis=0, reverse=reverse)
    prefix = inclusive - gathered
    spread = lax.all_to_all(prefix, "seq", 0, 0, tiled=True)
    return spread.reshape(-1, width)[:size].reshape(own_total.shape)


def lower_sum(own_total):
    return exclusive_scan(own_total, False)


def upper_sum(own_total):
    return exclusive_scan(own_total, True)


def natural(array):
    order = tuple(range(array.ndim - 3)) + (array.ndim - 2, array.ndim - 3, array.ndim - 1)
    return with_layout_constraint(array, Layout(order))


def body(query_raw, key_raw, value_raw, out_gain, out_grad):
    tok_rows, head_count, width = query_raw.shape
    blocks = tok_rows // GROUP
    blocked = (blocks, GROUP, head_count, width)
    query_act = jax.nn.silu(query_raw.astype(jnp.float32)).astype(jnp.bfloat16).reshape(blocked)
    key_act = jax.nn.silu(key_raw.astype(jnp.float32)).astype(jnp.bfloat16).reshape(blocked)
    value_blk = value_raw.reshape(blocked)
    mask = causal_mask(GROUP)[None, None]
    block_kv = jnp.einsum("cshd,cshe->chde", key_act, value_blk, preferred_element_type=jnp.float32)
    own_total = jnp.sum(block_kv, axis=0)
    before = lower_sum(own_total)
    if blocks == 1:
        state_b = before[None]
    else:
        state_b = before[None] + (jnp.cumsum(block_kv, axis=0) - block_kv)
    scores = jnp.einsum("cthd,cshd->chts", query_act, key_act, preferred_element_type=jnp.float32)
    attn = jnp.where(mask, scores, 0.0).astype(jnp.bfloat16)
    mixed = jnp.einsum("chts,cshe->cthe", attn, value_blk, preferred_element_type=jnp.float32)
    mixed = mixed + jnp.einsum(
        "cthd,chde->cthe", query_act, state_b, preferred_element_type=jnp.float32, precision=lax.Precision.HIGHEST
    )
    mixed = natural(mixed.reshape(tok_rows, head_count, width))
    grad_in = out_grad.astype(jnp.float32) * out_gain
    sq_part = jnp.sum(mixed * mixed, axis=(1, 2))
    cross_part = jnp.sum(grad_in * mixed, axis=(1, 2))
    both = jnp.stack([sq_part, cross_part])
    both = both + lax.ppermute(both, "head", [(0, 1), (1, 0)])
    sq_total, cross_total = both[0], both[1]
    features = head_count * width * lax.axis_size("head")
    inv_rms = lax.rsqrt(sq_total / features + 1e-06)
    normed_out = (mixed * inv_rms[:, None, None] * out_gain).astype(jnp.bfloat16)
    delta = (
        grad_in * inv_rms[:, None, None]
        - mixed * (cross_total * inv_rms**3 / features)[:, None, None]
    ).astype(jnp.bfloat16)
    delta_blk = delta.reshape(blocked)
    block_grad = jnp.einsum(
        "cthd,cthe->chde", query_act, delta_blk, preferred_element_type=jnp.float32
    )
    own_grad = jnp.sum(block_grad, axis=0)
    after = upper_sum(own_grad)
    if blocks == 1:
        grad_state = after[None]
    else:
        grad_state = after[None] + (lax.cumsum(block_grad, axis=0, reverse=True) - block_grad)
    bscore = jnp.einsum("cthe,cshe->chts", delta_blk, value_blk, preferred_element_type=jnp.float32)
    bscore = jnp.where(mask, bscore, 0.0).astype(jnp.bfloat16)
    dquery = jnp.einsum("chts,cshd->cthd", bscore, key_act, preferred_element_type=jnp.float32)
    dquery = dquery + jnp.einsum(
        "cthe,chde->cthd", delta_blk, state_b, preferred_element_type=jnp.float32, precision=lax.Precision.HIGHEST
    )
    dkey = jnp.einsum("chts,cthd->cshd", bscore, query_act, preferred_element_type=jnp.float32)
    dkey = dkey + jnp.einsum(
        "cshe,chde->cshd", value_blk, grad_state, preferred_element_type=jnp.float32, precision=lax.Precision.HIGHEST
    )
    dvalue = jnp.einsum("chts,cthe->cshe", attn, delta_blk, preferred_element_type=jnp.float32)
    dvalue = dvalue + jnp.einsum(
        "cshd,chde->cshe", key_act, grad_state, preferred_element_type=jnp.float32, precision=lax.Precision.HIGHEST
    )
    whole = (tok_rows, head_count, width)
    dquery, dkey, dvalue = natural(dquery), natural(dkey), natural(dvalue)
    query_grad = (dquery.reshape(whole) * silu_grad(query_raw.astype(jnp.float32))).astype(
        jnp.bfloat16
    )
    key_grad = (dkey.reshape(whole) * silu_grad(key_raw.astype(jnp.float32))).astype(jnp.bfloat16)
    value_grad = dvalue.reshape(whole).astype(jnp.bfloat16)
    return (normed_out, query_grad, key_grad, value_grad)


def solution(mesh):
    in_specs = (
        P("seq", "head", None),
        P("seq", "head", None),
        P("seq", "head", None),
        P("head", None),
        P("seq", "head", None),
    )
    out_specs = (
        P("seq", "head", None),
        P("seq", "head", None),
        P("seq", "head", None),
        P("seq", "head", None),
    )
    return jax.shard_map(body, mesh=mesh, in_specs=in_specs, out_specs=out_specs, check_vma=False)
```

```python
import jax
import jax.numpy as jnp
from jax import lax
from jax.sharding import PartitionSpec as P

GROUP = 256


def from_behind(shard, axis, by):
    count = lax.axis_size(axis)
    pairs = [(i, i + by) for i in range(count) if 0 <= i + by < count]
    return lax.ppermute(shard, axis, pairs)


def silu_grad(raw):
    sigma = jax.nn.sigmoid(raw)
    return sigma * (1.0 + raw * (1.0 - sigma))


def causal_mask(length):
    rows = lax.broadcasted_iota(jnp.int32, (length, length), 0)
    cols = lax.broadcasted_iota(jnp.int32, (length, length), 1)
    return cols <= rows


def exclusive_scan(own_total, reverse):
    count = lax.axis_size("seq")
    width = own_total.shape[-1]
    rows = own_total.reshape(-1, width)
    size = rows.shape[0]
    chunk = -(-size // count)
    rows = jnp.pad(rows, ((0, chunk * count - size), (0, 0)))
    gathered = lax.all_to_all(rows.reshape(count, chunk, width), "seq", 0, 0, tiled=True)
    inclusive = lax.cumsum(gathered, axis=0, reverse=reverse)
    prefix = inclusive - gathered
    spread = lax.all_to_all(prefix, "seq", 0, 0, tiled=True)
    return spread.reshape(-1, width)[:size].reshape(own_total.shape)


def lower_sum(own_total):
    return exclusive_scan(own_total, False)


def upper_sum(own_total):
    return exclusive_scan(own_total, True)


def body(query_raw, key_raw, value_raw, out_gain, out_grad):
    tok_rows, head_count, width = query_raw.shape
    blocks = tok_rows // GROUP
    blocked = (blocks, GROUP, head_count, width)
    query_act = jax.nn.silu(query_raw.astype(jnp.float32)).astype(jnp.bfloat16).reshape(blocked)
    key_act = jax.nn.silu(key_raw.astype(jnp.float32)).astype(jnp.bfloat16).reshape(blocked)
    value_blk = value_raw.reshape(blocked)
    mask = causal_mask(GROUP)[None, None]
    block_kv = jnp.einsum("cshd,cshe->chde", key_act, value_blk, preferred_element_type=jnp.float32)
    own_total = jnp.sum(block_kv, axis=0)
    before = lower_sum(own_total)
    if blocks == 1:
        state_b = lax.reduce_precision(before[None], 8, 7).astype(jnp.bfloat16)
    else:
        state_b = (before[None] + (jnp.cumsum(block_kv, axis=0) - block_kv)).astype(jnp.bfloat16)
    scores = jnp.einsum("cthd,cshd->chts", query_act, key_act, preferred_element_type=jnp.float32)
    attn = jnp.where(mask, scores, 0.0).astype(jnp.bfloat16)
    mixed = jnp.einsum("chts,cshe->cthe", attn, value_blk, preferred_element_type=jnp.float32)
    mixed = mixed + jnp.einsum(
        "cthd,chde->cthe", query_act, state_b, preferred_element_type=jnp.float32
    )
    mixed = mixed.reshape(tok_rows, head_count, width)
    grad_in = out_grad.astype(jnp.float32) * out_gain
    sq_part = jnp.sum(mixed * mixed, axis=(1, 2))
    cross_part = jnp.sum(grad_in * mixed, axis=(1, 2))
    both = jnp.stack([sq_part, cross_part])
    both = both + lax.ppermute(both, "head", [(0, 1), (1, 0)])
    sq_total, cross_total = both[0], both[1]
    features = head_count * width * lax.axis_size("head")
    inv_rms = lax.rsqrt(sq_total / features + 1e-06)
    normed_out = (mixed * inv_rms[:, None, None] * out_gain).astype(jnp.bfloat16)
    delta = (
        grad_in * inv_rms[:, None, None]
        - mixed * (cross_total * inv_rms**3 / features)[:, None, None]
    ).astype(jnp.bfloat16)
    delta_blk = delta.reshape(blocked)
    block_grad = jnp.einsum(
        "cthd,cthe->chde", query_act, delta_blk, preferred_element_type=jnp.float32
    )
    own_grad = jnp.sum(block_grad, axis=0)
    after = upper_sum(own_grad)
    if blocks == 1:
        grad_state = lax.reduce_precision(after[None], 8, 7).astype(jnp.bfloat16)
    else:
        grad_state = (after[None] + (lax.cumsum(block_grad, axis=0, reverse=True) - block_grad)).astype(jnp.bfloat16)
    bscore = jnp.einsum("cthe,cshe->chts", delta_blk, value_blk, preferred_element_type=jnp.float32)
    bscore = jnp.where(mask, bscore, 0.0).astype(jnp.bfloat16)
    dquery = jnp.einsum("chts,cshd->cthd", bscore, key_act, preferred_element_type=jnp.float32)
    dquery = dquery + jnp.einsum(
        "cthe,chde->cthd", delta_blk, state_b, preferred_element_type=jnp.float32
    )
    dkey = jnp.einsum("chts,cthd->cshd", bscore, query_act, preferred_element_type=jnp.float32)
    dkey = dkey + jnp.einsum(
        "cshe,chde->cshd", value_blk, grad_state, preferred_element_type=jnp.float32
    )
    dvalue = jnp.einsum("chts,cthe->cshe", attn, delta_blk, preferred_element_type=jnp.float32)
    dvalue = dvalue + jnp.einsum(
        "cshd,chde->cshe", key_act, grad_state, preferred_element_type=jnp.float32
    )
    whole = (tok_rows, head_count, width)
    query_grad = (dquery.reshape(whole) * silu_grad(query_raw.astype(jnp.float32))).astype(
        jnp.bfloat16
    )
    key_grad = (dkey.reshape(whole) * silu_grad(key_raw.astype(jnp.float32))).astype(jnp.bfloat16)
    value_grad = dvalue.reshape(whole).astype(jnp.bfloat16)
    return (normed_out, query_grad, key_grad, value_grad)


def solution(mesh):
    in_specs = (
        P("seq", "head", None),
        P("seq", "head", None),
        P("seq", "head", None),
        P("head", None),
        P("seq", "head", None),
    )
    out_specs = (
        P("seq", "head", None),
        P("seq", "head", None),
        P("seq", "head", None),
        P("seq", "head", None),
    )
    return jax.shard_map(body, mesh=mesh, in_specs=in_specs, out_specs=out_specs, check_vma=False)
```

```python
import jax
import jax.numpy as jnp
from jax import lax
from jax.sharding import PartitionSpec as P

GROUP = 256


def from_behind(shard, axis, by):
    count = lax.axis_size(axis)
    pairs = [(i, i + by) for i in range(count) if 0 <= i + by < count]
    return lax.ppermute(shard, axis, pairs)


def silu_grad(raw):
    sigma = jax.nn.sigmoid(raw)
    return sigma * (1.0 + raw * (1.0 - sigma))


def causal_mask(length):
    rows = lax.broadcasted_iota(jnp.int32, (length, length), 0)
    cols = lax.broadcasted_iota(jnp.int32, (length, length), 1)
    return cols <= rows


def exclusive_scan(own_total, reverse):
    count = lax.axis_size("seq")
    width = own_total.shape[-1]
    rows = own_total.reshape(-1, width)
    size = rows.shape[0]
    chunk = -(-size // count)
    rows = jnp.pad(rows, ((0, chunk * count - size), (0, 0)))
    gathered = lax.all_to_all(rows.reshape(count, chunk, width), "seq", 0, 0, tiled=True)
    if count > 32:
        prefix = lax.cumsum(gathered, axis=0, reverse=reverse) - gathered
    else:
        order = range(count - 1, -1, -1) if reverse else range(count)
        running = jnp.zeros_like(gathered[:1])
        parts = [None] * count
        for index in order:
            parts[index] = running
            running = running + gathered[index:index + 1]
        prefix = jnp.concatenate(parts, axis=0)
    spread = lax.all_to_all(prefix, "seq", 0, 0, tiled=True)
    return spread.reshape(-1, width)[:size].reshape(own_total.shape)


def lower_sum(own_total):
    return exclusive_scan(own_total, False)


def upper_sum(own_total):
    return exclusive_scan(own_total, True)


def body(query_raw, key_raw, value_raw, out_gain, out_grad):
    tok_rows, head_count, width = query_raw.shape
    blocks = tok_rows // GROUP
    blocked = (blocks, GROUP, head_count, width)
    query_act = jax.nn.silu(query_raw.astype(jnp.float32)).astype(jnp.bfloat16).reshape(blocked)
    key_act = jax.nn.silu(key_raw.astype(jnp.float32)).astype(jnp.bfloat16).reshape(blocked)
    value_blk = value_raw.reshape(blocked)
    mask = causal_mask(GROUP)[None, None]
    block_kv = jnp.einsum("cshd,cshe->chde", key_act, value_blk, preferred_element_type=jnp.float32)
    own_total = jnp.sum(block_kv, axis=0)
    before = lower_sum(own_total)
    if blocks == 1:
        state_b = lax.reduce_precision(before[None], 8, 7).astype(jnp.bfloat16)
    else:
        state_b = (before[None] + (jnp.cumsum(block_kv, axis=0) - block_kv)).astype(jnp.bfloat16)
    scores = jnp.einsum("cthd,cshd->chts", query_act, key_act, preferred_element_type=jnp.float32)
    attn = jnp.where(mask, scores, 0.0).astype(jnp.bfloat16)
    mixed = jnp.einsum("chts,cshe->cthe", attn, value_blk, preferred_element_type=jnp.float32)
    mixed = mixed + jnp.einsum(
        "cthd,chde->cthe", query_act, state_b, preferred_element_type=jnp.float32
    )
    mixed = mixed.reshape(tok_rows, head_count, width)
    grad_in = out_grad.astype(jnp.float32) * out_gain
    sq_part = jnp.sum(mixed * mixed, axis=(1, 2))
    cross_part = jnp.sum(grad_in * mixed, axis=(1, 2))
    both = jnp.stack([sq_part, cross_part])
    both = both + lax.ppermute(both, "head", [(0, 1), (1, 0)])
    sq_total, cross_total = both[0], both[1]
    features = head_count * width * lax.axis_size("head")
    inv_rms = lax.rsqrt(sq_total / features + 1e-06)
    normed_out = (mixed * inv_rms[:, None, None] * out_gain).astype(jnp.bfloat16)
    delta = (
        grad_in * inv_rms[:, None, None]
        - mixed * (cross_total * inv_rms**3 / features)[:, None, None]
    ).astype(jnp.bfloat16)
    delta_blk = delta.reshape(blocked)
    block_grad = jnp.einsum(
        "cthd,cthe->chde", query_act, delta_blk, preferred_element_type=jnp.float32
    )
    own_grad = jnp.sum(block_grad, axis=0)
    after = upper_sum(own_grad)
    if blocks == 1:
        grad_state = lax.reduce_precision(after[None], 8, 7).astype(jnp.bfloat16)
    else:
        grad_state = (after[None] + (lax.cumsum(block_grad, axis=0, reverse=True) - block_grad)).astype(jnp.bfloat16)
    bscore = jnp.einsum("cthe,cshe->chts", delta_blk, value_blk, preferred_element_type=jnp.float32)
    bscore = jnp.where(mask, bscore, 0.0).astype(jnp.bfloat16)
    dquery = jnp.einsum("chts,cshd->cthd", bscore, key_act, preferred_element_type=jnp.float32)
    dquery = dquery + jnp.einsum(
        "cthe,chde->cthd", delta_blk, state_b, preferred_element_type=jnp.float32
    )
    dkey = jnp.einsum("chts,cthd->cshd", bscore, query_act, preferred_element_type=jnp.float32)
    dkey = dkey + jnp.einsum(
        "cshe,chde->cshd", value_blk, grad_state, preferred_element_type=jnp.float32
    )
    dvalue = jnp.einsum("chts,cthe->cshe", attn, delta_blk, preferred_element_type=jnp.float32)
    dvalue = dvalue + jnp.einsum(
        "cshd,chde->cshe", key_act, grad_state, preferred_element_type=jnp.float32
    )
    whole = (tok_rows, head_count, width)
    query_grad = (dquery.reshape(whole) * silu_grad(query_raw.astype(jnp.float32))).astype(
        jnp.bfloat16
    )
    key_grad = (dkey.reshape(whole) * silu_grad(key_raw.astype(jnp.float32))).astype(jnp.bfloat16)
    value_grad = dvalue.reshape(whole).astype(jnp.bfloat16)
    return (normed_out, query_grad, key_grad, value_grad)


def solution(mesh):
    in_specs = (
        P("seq", "head", None),
        P("seq", "head", None),
        P("seq", "head", None),
        P("head", None),
        P("seq", "head", None),
    )
    out_specs = (
        P("seq", "head", None),
        P("seq", "head", None),
        P("seq", "head", None),
        P("seq", "head", None),
    )
    return jax.shard_map(body, mesh=mesh, in_specs=in_specs, out_specs=out_specs, check_vma=False)
```

```python
import jax
import jax.numpy as jnp
from jax import lax
from jax.sharding import PartitionSpec as P

GROUP = 256


def from_behind(shard, axis, by):
    count = lax.axis_size(axis)
    pairs = [(i, i + by) for i in range(count) if 0 <= i + by < count]
    return lax.ppermute(shard, axis, pairs)


def silu_grad(raw):
    sigma = jax.nn.sigmoid(raw)
    return sigma * (1.0 + raw * (1.0 - sigma))


def causal_mask(length):
    rows = lax.broadcasted_iota(jnp.int32, (length, length), 0)
    cols = lax.broadcasted_iota(jnp.int32, (length, length), 1)
    return cols <= rows


def exclusive_scan(own_total, reverse):
    count = lax.axis_size("seq")
    width = own_total.shape[-1]
    rows = own_total.reshape(-1, width)
    size = rows.shape[0]
    chunk = -(-size // count)
    rows = jnp.pad(rows, ((0, chunk * count - size), (0, 0)))
    gathered = lax.all_to_all(rows.reshape(count, chunk, width), "seq", 0, 0, tiled=True)
    if count > 32:
        prefix = lax.cumsum(gathered, axis=0, reverse=reverse) - gathered
    else:
        rows_i = lax.broadcasted_iota(jnp.int32, (count, count, 1, 1), 0)
        cols_i = lax.broadcasted_iota(jnp.int32, (count, count, 1, 1), 1)
        earlier = (cols_i > rows_i) if reverse else (cols_i < rows_i)
        prefix = jnp.sum(jnp.where(earlier, gathered[None], 0.0), axis=1)
    spread = lax.all_to_all(prefix, "seq", 0, 0, tiled=True)
    return spread.reshape(-1, width)[:size].reshape(own_total.shape)


def lower_sum(own_total):
    return exclusive_scan(own_total, False)


def upper_sum(own_total):
    return exclusive_scan(own_total, True)


def body(query_raw, key_raw, value_raw, out_gain, out_grad):
    tok_rows, head_count, width = query_raw.shape
    blocks = tok_rows // GROUP
    blocked = (blocks, GROUP, head_count, width)
    query_act = jax.nn.silu(query_raw.astype(jnp.float32)).astype(jnp.bfloat16).reshape(blocked)
    key_act = jax.nn.silu(key_raw.astype(jnp.float32)).astype(jnp.bfloat16).reshape(blocked)
    value_blk = value_raw.reshape(blocked)
    mask = causal_mask(GROUP)[None, None]
    block_kv = jnp.einsum("cshd,cshe->chde", key_act, value_blk, preferred_element_type=jnp.float32)
    own_total = jnp.sum(block_kv, axis=0)
    before = lower_sum(own_total)
    if blocks == 1:
        state_b = lax.reduce_precision(before[None], 8, 7).astype(jnp.bfloat16)
    else:
        state_b = (before[None] + (jnp.cumsum(block_kv, axis=0) - block_kv)).astype(jnp.bfloat16)
    scores = jnp.einsum("cthd,cshd->chts", query_act, key_act, preferred_element_type=jnp.float32)
    attn = jnp.where(mask, scores, 0.0).astype(jnp.bfloat16)
    mixed = jnp.einsum("chts,cshe->cthe", attn, value_blk, preferred_element_type=jnp.float32)
    mixed = mixed + jnp.einsum(
        "cthd,chde->cthe", query_act, state_b, preferred_element_type=jnp.float32
    )
    mixed = mixed.reshape(tok_rows, head_count, width)
    grad_in = out_grad.astype(jnp.float32) * out_gain
    sq_part = jnp.sum(mixed * mixed, axis=(1, 2))
    cross_part = jnp.sum(grad_in * mixed, axis=(1, 2))
    both = jnp.stack([sq_part, cross_part])
    both = both + lax.ppermute(both, "head", [(0, 1), (1, 0)])
    sq_total, cross_total = both[0], both[1]
    features = head_count * width * lax.axis_size("head")
    inv_rms = lax.rsqrt(sq_total / features + 1e-06)
    normed_out = (mixed * inv_rms[:, None, None] * out_gain).astype(jnp.bfloat16)
    delta = (
        grad_in * inv_rms[:, None, None]
        - mixed * (cross_total * inv_rms**3 / features)[:, None, None]
    ).astype(jnp.bfloat16)
    delta_blk = delta.reshape(blocked)
    block_grad = jnp.einsum(
        "cthd,cthe->chde", query_act, delta_blk, preferred_element_type=jnp.float32
    )
    own_grad = jnp.sum(block_grad, axis=0)
    after = upper_sum(own_grad)
    if blocks == 1:
        grad_state = lax.reduce_precision(after[None], 8, 7).astype(jnp.bfloat16)
    else:
        grad_state = (after[None] + (lax.cumsum(block_grad, axis=0, reverse=True) - block_grad)).astype(jnp.bfloat16)
    bscore = jnp.einsum("cthe,cshe->chts", delta_blk, value_blk, preferred_element_type=jnp.float32)
    bscore = jnp.where(mask, bscore, 0.0).astype(jnp.bfloat16)
    dquery = jnp.einsum("chts,cshd->cthd", bscore, key_act, preferred_element_type=jnp.float32)
    dquery = dquery + jnp.einsum(
        "cthe,chde->cthd", delta_blk, state_b, preferred_element_type=jnp.float32
    )
    dkey = jnp.einsum("chts,cthd->cshd", bscore, query_act, preferred_element_type=jnp.float32)
    dkey = dkey + jnp.einsum(
        "cshe,chde->cshd", value_blk, grad_state, preferred_element_type=jnp.float32
    )
    dvalue = jnp.einsum("chts,cthe->cshe", attn, delta_blk, preferred_element_type=jnp.float32)
    dvalue = dvalue + jnp.einsum(
        "cshd,chde->cshe", key_act, grad_state, preferred_element_type=jnp.float32
    )
    whole = (tok_rows, head_count, width)
    query_grad = (dquery.reshape(whole) * silu_grad(query_raw.astype(jnp.float32))).astype(
        jnp.bfloat16
    )
    key_grad = (dkey.reshape(whole) * silu_grad(key_raw.astype(jnp.float32))).astype(jnp.bfloat16)
    value_grad = dvalue.reshape(whole).astype(jnp.bfloat16)
    return (normed_out, query_grad, key_grad, value_grad)


def solution(mesh):
    in_specs = (
        P("seq", "head", None),
        P("seq", "head", None),
        P("seq", "head", None),
        P("head", None),
        P("seq", "head", None),
    )
    out_specs = (
        P("seq", "head", None),
        P("seq", "head", None),
        P("seq", "head", None),
        P("seq", "head", None),
    )
    return jax.shard_map(body, mesh=mesh, in_specs=in_specs, out_specs=out_specs, check_vma=False)
```

```python
import jax
import jax.numpy as jnp
from jax import lax
from jax.sharding import PartitionSpec as P
from jax.experimental.layout import Layout, with_layout_constraint

GROUP = 256


def from_behind(shard, axis, by):
    count = lax.axis_size(axis)
    pairs = [(i, i + by) for i in range(count) if 0 <= i + by < count]
    return lax.ppermute(shard, axis, pairs)


def silu_grad(raw):
    sigma = jax.nn.sigmoid(raw)
    return sigma * (1.0 + raw * (1.0 - sigma))


def causal_mask(length):
    rows = lax.broadcasted_iota(jnp.int32, (length, length), 0)
    cols = lax.broadcasted_iota(jnp.int32, (length, length), 1)
    return cols <= rows


def exclusive_scan(own_total, reverse):
    count = lax.axis_size("seq")
    width = own_total.shape[-1]
    rows = own_total.reshape(-1, width)
    size = rows.shape[0]
    chunk = -(-size // count)
    rows = jnp.pad(rows, ((0, chunk * count - size), (0, 0)))
    gathered = lax.all_to_all(rows.reshape(count, chunk, width), "seq", 0, 0, tiled=True)
    inclusive = lax.cumsum(gathered, axis=0, reverse=reverse)
    prefix = inclusive - gathered
    spread = lax.all_to_all(prefix, "seq", 0, 0, tiled=True)
    return spread.reshape(-1, width)[:size].reshape(own_total.shape)


def lower_sum(own_total):
    return exclusive_scan(own_total, False)


def upper_sum(own_total):
    return exclusive_scan(own_total, True)


def head_major(array):
    order = tuple(range(array.ndim - 3)) + (array.ndim - 2, array.ndim - 3, array.ndim - 1)
    return with_layout_constraint(array, Layout(order))


def body(query_raw, key_raw, value_raw, out_gain, out_grad):
    tok_rows, head_count, width = query_raw.shape
    blocks = tok_rows // GROUP
    blocked = (blocks, GROUP, head_count, width)
    query_act = head_major(jax.nn.silu(query_raw.astype(jnp.float32)).astype(jnp.bfloat16).reshape(blocked))
    key_act = head_major(jax.nn.silu(key_raw.astype(jnp.float32)).astype(jnp.bfloat16).reshape(blocked))
    value_blk = value_raw.reshape(blocked)
    mask = causal_mask(GROUP)[None, None]
    block_kv = jnp.einsum("cshd,cshe->chde", key_act, value_blk, preferred_element_type=jnp.float32)
    own_total = jnp.sum(block_kv, axis=0)
    before = lower_sum(own_total)
    if blocks == 1:
        state_b = lax.reduce_precision(before[None], 8, 7).astype(jnp.bfloat16)
    else:
        state_b = (before[None] + (jnp.cumsum(block_kv, axis=0) - block_kv)).astype(jnp.bfloat16)
    scores = jnp.einsum("cthd,cshd->chts", query_act, key_act, preferred_element_type=jnp.float32)
    attn = jnp.where(mask, scores, 0.0).astype(jnp.bfloat16)
    mixed = jnp.einsum("chts,cshe->cthe", attn, value_blk, preferred_element_type=jnp.float32)
    mixed = mixed + jnp.einsum(
        "cthd,chde->cthe", query_act, state_b, preferred_element_type=jnp.float32
    )
    mixed = mixed.reshape(tok_rows, head_count, width)
    grad_in = out_grad.astype(jnp.float32) * out_gain
    sq_part = jnp.sum(mixed * mixed, axis=(1, 2))
    cross_part = jnp.sum(grad_in * mixed, axis=(1, 2))
    both = jnp.stack([sq_part, cross_part])
    both = both + lax.ppermute(both, "head", [(0, 1), (1, 0)])
    sq_total, cross_total = both[0], both[1]
    features = head_count * width * lax.axis_size("head")
    inv_rms = lax.rsqrt(sq_total / features + 1e-06)
    normed_out = (mixed * inv_rms[:, None, None] * out_gain).astype(jnp.bfloat16)
    delta = (
        grad_in * inv_rms[:, None, None]
        - mixed * (cross_total * inv_rms**3 / features)[:, None, None]
    ).astype(jnp.bfloat16)
    delta_blk = head_major(delta.reshape(blocked))
    block_grad = jnp.einsum(
        "cthd,cthe->chde", query_act, delta_blk, preferred_element_type=jnp.float32
    )
    own_grad = jnp.sum(block_grad, axis=0)
    after = upper_sum(own_grad)
    if blocks == 1:
        grad_state = lax.reduce_precision(after[None], 8, 7).astype(jnp.bfloat16)
    else:
        grad_state = (after[None] + (lax.cumsum(block_grad, axis=0, reverse=True) - block_grad)).astype(jnp.bfloat16)
    bscore = jnp.einsum("cthe,cshe->chts", delta_blk, value_blk, preferred_element_type=jnp.float32)
    bscore = jnp.where(mask, bscore, 0.0).astype(jnp.bfloat16)
    dquery = jnp.einsum("chts,cshd->cthd", bscore, key_act, preferred_element_type=jnp.float32)
    dquery = dquery + jnp.einsum(
        "cthe,chde->cthd", delta_blk, state_b, preferred_element_type=jnp.float32
    )
    dkey = jnp.einsum("chts,cthd->cshd", bscore, query_act, preferred_element_type=jnp.float32)
    dkey = dkey + jnp.einsum(
        "cshe,chde->cshd", value_blk, grad_state, preferred_element_type=jnp.float32
    )
    dvalue = jnp.einsum("chts,cthe->cshe", attn, delta_blk, preferred_element_type=jnp.float32)
    dvalue = dvalue + jnp.einsum(
        "cshd,chde->cshe", key_act, grad_state, preferred_element_type=jnp.float32
    )
    whole = (tok_rows, head_count, width)
    query_grad = (dquery.reshape(whole) * silu_grad(query_raw.astype(jnp.float32))).astype(
        jnp.bfloat16
    )
    key_grad = (dkey.reshape(whole) * silu_grad(key_raw.astype(jnp.float32))).astype(jnp.bfloat16)
    value_grad = dvalue.reshape(whole).astype(jnp.bfloat16)
    return (normed_out, query_grad, key_grad, value_grad)


def solution(mesh):
    in_specs = (
        P("seq", "head", None),
        P("seq", "head", None),
        P("seq", "head", None),
        P("head", None),
        P("seq", "head", None),
    )
    out_specs = (
        P("seq", "head", None),
        P("seq", "head", None),
        P("seq", "head", None),
        P("seq", "head", None),
    )
    return jax.shard_map(body, mesh=mesh, in_specs=in_specs, out_specs=out_specs, check_vma=False)
```

```python
import jax
import jax.numpy as jnp
from jax import lax
from jax.sharding import PartitionSpec as P

GROUP = 256


def from_behind(shard, axis, by):
    count = lax.axis_size(axis)
    pairs = [(i, i + by) for i in range(count) if 0 <= i + by < count]
    return lax.ppermute(shard, axis, pairs)


def silu_grad(raw):
    sigma = jax.nn.sigmoid(raw)
    return sigma * (1.0 + raw * (1.0 - sigma))


def causal_mask(length):
    rows = lax.broadcasted_iota(jnp.int32, (length, length), 0)
    cols = lax.broadcasted_iota(jnp.int32, (length, length), 1)
    return cols <= rows


def exclusive_scan(own_total, reverse, early=None, late=None):
    count = lax.axis_size("seq")
    width = own_total.shape[-1]
    rows = own_total.reshape(-1, width)
    size = rows.shape[0]
    chunk = -(-size // count)
    rows = jnp.pad(rows, ((0, chunk * count - size), (0, 0)))
    gathered = lax.all_to_all(rows.reshape(count, chunk, width), "seq", 0, 0, tiled=True)
    if early is not None:
        gathered, early = lax.optimization_barrier((gathered, early))
    inclusive = lax.cumsum(gathered, axis=0, reverse=reverse)
    prefix = inclusive - gathered
    if late is not None:
        prefix, late = lax.optimization_barrier((prefix, late))
    spread = lax.all_to_all(prefix, "seq", 0, 0, tiled=True)
    spread = spread.reshape(-1, width)[:size].reshape(own_total.shape)
    if early is None:
        return spread
    return spread, early, late


def lower_sum(own_total):
    return exclusive_scan(own_total, False)


def upper_sum(own_total, early, late):
    return exclusive_scan(own_total, True, early, late)


def body(query_raw, key_raw, value_raw, out_gain, out_grad):
    tok_rows, head_count, width = query_raw.shape
    blocks = tok_rows // GROUP
    blocked = (blocks, GROUP, head_count, width)
    query_act = jax.nn.silu(query_raw.astype(jnp.float32)).astype(jnp.bfloat16).reshape(blocked)
    key_act = jax.nn.silu(key_raw.astype(jnp.float32)).astype(jnp.bfloat16).reshape(blocked)
    value_blk = value_raw.reshape(blocked)
    mask = causal_mask(GROUP)[None, None]
    block_kv = jnp.einsum("cshd,cshe->chde", key_act, value_blk, preferred_element_type=jnp.float32)
    own_total = jnp.sum(block_kv, axis=0)
    before = lower_sum(own_total)
    if blocks == 1:
        state_b = lax.reduce_precision(before[None], 8, 7).astype(jnp.bfloat16)
    else:
        state_b = (before[None] + (jnp.cumsum(block_kv, axis=0) - block_kv)).astype(jnp.bfloat16)
    scores = jnp.einsum("cthd,cshd->chts", query_act, key_act, preferred_element_type=jnp.float32)
    attn = jnp.where(mask, scores, 0.0).astype(jnp.bfloat16)
    mixed = jnp.einsum("chts,cshe->cthe", attn, value_blk, preferred_element_type=jnp.float32)
    mixed = mixed + jnp.einsum(
        "cthd,chde->cthe", query_act, state_b, preferred_element_type=jnp.float32
    )
    mixed = mixed.reshape(tok_rows, head_count, width)
    grad_in = out_grad.astype(jnp.float32) * out_gain
    sq_part = jnp.sum(mixed * mixed, axis=(1, 2))
    cross_part = jnp.sum(grad_in * mixed, axis=(1, 2))
    both = jnp.stack([sq_part, cross_part])
    both = both + lax.ppermute(both, "head", [(0, 1), (1, 0)])
    sq_total, cross_total = both[0], both[1]
    features = head_count * width * lax.axis_size("head")
    inv_rms = lax.rsqrt(sq_total / features + 1e-06)
    delta = (
        grad_in * inv_rms[:, None, None]
        - mixed * (cross_total * inv_rms**3 / features)[:, None, None]
    ).astype(jnp.bfloat16)
    delta_blk = delta.reshape(blocked)
    block_grad = jnp.einsum(
        "cthd,cthe->chde", query_act, delta_blk, preferred_element_type=jnp.float32
    )
    own_grad = jnp.sum(block_grad, axis=0)
    normed_out = (mixed * inv_rms[:, None, None] * out_gain).astype(jnp.bfloat16)
    after, delta_late, _ = upper_sum(own_grad, delta_blk, None)
    if blocks == 1:
        grad_state = lax.reduce_precision(after[None], 8, 7).astype(jnp.bfloat16)
    else:
        grad_state = (after[None] + (lax.cumsum(block_grad, axis=0, reverse=True) - block_grad)).astype(jnp.bfloat16)
    bscore = jnp.einsum("cthe,cshe->chts", delta_late, value_blk, preferred_element_type=jnp.float32)
    bscore = jnp.where(mask, bscore, 0.0).astype(jnp.bfloat16)
    dquery = jnp.einsum("chts,cshd->cthd", bscore, key_act, preferred_element_type=jnp.float32)
    dquery = dquery + jnp.einsum(
        "cthe,chde->cthd", delta_blk, state_b, preferred_element_type=jnp.float32
    )
    dkey = jnp.einsum("chts,cthd->cshd", bscore, query_act, preferred_element_type=jnp.float32)
    dkey = dkey + jnp.einsum(
        "cshe,chde->cshd", value_blk, grad_state, preferred_element_type=jnp.float32
    )
    dvalue = jnp.einsum("chts,cthe->cshe", attn, delta_blk, preferred_element_type=jnp.float32)
    dvalue = dvalue + jnp.einsum(
        "cshd,chde->cshe", key_act, grad_state, preferred_element_type=jnp.float32
    )
    whole = (tok_rows, head_count, width)
    query_grad = (dquery.reshape(whole) * silu_grad(query_raw.astype(jnp.float32))).astype(
        jnp.bfloat16
    )
    key_grad = (dkey.reshape(whole) * silu_grad(key_raw.astype(jnp.float32))).astype(jnp.bfloat16)
    value_grad = dvalue.reshape(whole).astype(jnp.bfloat16)
    return (normed_out, query_grad, key_grad, value_grad)


def solution(mesh):
    in_specs = (
        P("seq", "head", None),
        P("seq", "head", None),
        P("seq", "head", None),
        P("head", None),
        P("seq", "head", None),
    )
    out_specs = (
        P("seq", "head", None),
        P("seq", "head", None),
        P("seq", "head", None),
        P("seq", "head", None),
    )
    return jax.shard_map(body, mesh=mesh, in_specs=in_specs, out_specs=out_specs, check_vma=False)
```

```python
import jax
import jax.numpy as jnp
from jax import lax
from jax.sharding import PartitionSpec as P

GROUP = 256


def from_behind(shard, axis, by):
    count = lax.axis_size(axis)
    pairs = [(i, i + by) for i in range(count) if 0 <= i + by < count]
    return lax.ppermute(shard, axis, pairs)


def silu_grad(raw):
    sigma = jax.nn.sigmoid(raw)
    return sigma * (1.0 + raw * (1.0 - sigma))


def causal_mask(length):
    rows = lax.broadcasted_iota(jnp.int32, (length, length), 0)
    cols = lax.broadcasted_iota(jnp.int32, (length, length), 1)
    return cols <= rows


def exclusive_scan(own_total, reverse, early=None, late=None):
    count = lax.axis_size("seq")
    width = own_total.shape[-1]
    rows = own_total.reshape(-1, width)
    size = rows.shape[0]
    chunk = -(-size // count)
    rows = jnp.pad(rows, ((0, chunk * count - size), (0, 0)))
    gathered = lax.all_to_all(rows.reshape(count, chunk, width), "seq", 0, 0, tiled=True)
    if early is not None:
        gathered, early = lax.optimization_barrier((gathered, early))
    inclusive = lax.cumsum(gathered, axis=0, reverse=reverse)
    prefix = inclusive - gathered
    if late is not None:
        prefix, late = lax.optimization_barrier((prefix, late))
    spread = lax.all_to_all(prefix, "seq", 0, 0, tiled=True)
    spread = spread.reshape(-1, width)[:size].reshape(own_total.shape)
    if early is None:
        return spread
    return spread, early, late


def lower_sum(own_total):
    return exclusive_scan(own_total, False)


def upper_sum(own_total, early, late):
    return exclusive_scan(own_total, True, early, late)


def body(query_raw, key_raw, value_raw, out_gain, out_grad):
    tok_rows, head_count, width = query_raw.shape
    blocks = tok_rows // GROUP
    blocked = (blocks, GROUP, head_count, width)
    query_act = jax.nn.silu(query_raw.astype(jnp.float32)).astype(jnp.bfloat16).reshape(blocked)
    key_act = jax.nn.silu(key_raw.astype(jnp.float32)).astype(jnp.bfloat16).reshape(blocked)
    value_blk = value_raw.reshape(blocked)
    mask = causal_mask(GROUP)[None, None]
    block_kv = jnp.einsum("cshd,cshe->chde", key_act, value_blk, preferred_element_type=jnp.float32)
    own_total = jnp.sum(block_kv, axis=0)
    before = lower_sum(own_total)
    if blocks == 1:
        state_b = lax.reduce_precision(before[None], 8, 7).astype(jnp.bfloat16)
    else:
        state_b = (before[None] + (jnp.cumsum(block_kv, axis=0) - block_kv)).astype(jnp.bfloat16)
    scores = jnp.einsum("cthd,cshd->chts", query_act, key_act, preferred_element_type=jnp.float32)
    attn = jnp.where(mask, scores, 0.0).astype(jnp.bfloat16)
    mixed = jnp.einsum("chts,cshe->cthe", attn, value_blk, preferred_element_type=jnp.float32)
    mixed = mixed + jnp.einsum(
        "cthd,chde->cthe", query_act, state_b, preferred_element_type=jnp.float32
    )
    mixed = mixed.reshape(tok_rows, head_count, width)
    grad_in = out_grad.astype(jnp.float32) * out_gain
    sq_part = jnp.sum(mixed * mixed, axis=(1, 2))
    cross_part = jnp.sum(grad_in * mixed, axis=(1, 2))
    both = jnp.stack([sq_part, cross_part])
    both = both + lax.ppermute(both, "head", [(0, 1), (1, 0)])
    sq_total, cross_total = both[0], both[1]
    features = head_count * width * lax.axis_size("head")
    inv_rms = lax.rsqrt(sq_total / features + 1e-06)
    delta_f32 = (
        grad_in * inv_rms[:, None, None]
        - mixed * (cross_total * inv_rms**3 / features)[:, None, None]
    )
    delta = delta_f32.astype(jnp.bfloat16)
    delta_blk = delta.reshape(blocked)
    block_grad = jnp.einsum(
        "cthd,cthe->chde", query_act.astype(jnp.float32), delta_f32.reshape(blocked),
        preferred_element_type=jnp.float32, precision=lax.Precision.HIGHEST,
    )
    own_grad = jnp.sum(block_grad, axis=0)
    normed_out = (mixed * inv_rms[:, None, None] * out_gain).astype(jnp.bfloat16)
    after, delta_late, _ = upper_sum(own_grad, delta_blk, None)
    if blocks == 1:
        grad_state = lax.reduce_precision(after[None], 8, 7).astype(jnp.bfloat16)
    else:
        grad_state = (after[None] + (lax.cumsum(block_grad, axis=0, reverse=True) - block_grad)).astype(jnp.bfloat16)
    bscore = jnp.einsum("cthe,cshe->chts", delta_late, value_blk, preferred_element_type=jnp.float32)
    bscore = jnp.where(mask, bscore, 0.0).astype(jnp.bfloat16)
    dquery = jnp.einsum("chts,cshd->cthd", bscore, key_act, preferred_element_type=jnp.float32)
    dquery = dquery + jnp.einsum(
        "cthe,chde->cthd", delta_blk, state_b, preferred_element_type=jnp.float32
    )
    dkey = jnp.einsum("chts,cthd->cshd", bscore, query_act, preferred_element_type=jnp.float32)
    dkey = dkey + jnp.einsum(
        "cshe,chde->cshd", value_blk, grad_state, preferred_element_type=jnp.float32
    )
    dvalue = jnp.einsum("chts,cthe->cshe", attn, delta_blk, preferred_element_type=jnp.float32)
    dvalue = dvalue + jnp.einsum(
        "cshd,chde->cshe", key_act, grad_state, preferred_element_type=jnp.float32
    )
    whole = (tok_rows, head_count, width)
    query_grad = (dquery.reshape(whole) * silu_grad(query_raw.astype(jnp.float32))).astype(
        jnp.bfloat16
    )
    key_grad = (dkey.reshape(whole) * silu_grad(key_raw.astype(jnp.float32))).astype(jnp.bfloat16)
    value_grad = dvalue.reshape(whole).astype(jnp.bfloat16)
    return (normed_out, query_grad, key_grad, value_grad)


def solution(mesh):
    in_specs = (
        P("seq", "head", None),
        P("seq", "head", None),
        P("seq", "head", None),
        P("head", None),
        P("seq", "head", None),
    )
    out_specs = (
        P("seq", "head", None),
        P("seq", "head", None),
        P("seq", "head", None),
        P("seq", "head", None),
    )
    return jax.shard_map(body, mesh=mesh, in_specs=in_specs, out_specs=out_specs, check_vma=False)
```

```python
import jax
import jax.numpy as jnp
from jax import lax
from jax.sharding import PartitionSpec as P

GROUP = 256


def from_behind(shard, axis, by):
    count = lax.axis_size(axis)
    pairs = [(i, i + by) for i in range(count) if 0 <= i + by < count]
    return lax.ppermute(shard, axis, pairs)


def silu_grad(raw):
    sigma = jax.nn.sigmoid(raw)
    return sigma * (1.0 + raw * (1.0 - sigma))


def causal_mask(length):
    rows = lax.broadcasted_iota(jnp.int32, (length, length), 0)
    cols = lax.broadcasted_iota(jnp.int32, (length, length), 1)
    return cols <= rows


def exclusive_scan(own_total, reverse, early=None, late=None):
    count = lax.axis_size("seq")
    width = own_total.shape[-1]
    rows = own_total.reshape(-1, width)
    size = rows.shape[0]
    chunk = -(-size // count)
    rows = jnp.pad(rows, ((0, chunk * count - size), (0, 0)))
    gathered = lax.all_to_all(rows.reshape(count, chunk, width), "seq", 0, 0, tiled=True)
    if early is not None:
        gathered, early = lax.optimization_barrier((gathered, early))
    inclusive = lax.cumsum(gathered, axis=0, reverse=reverse)
    prefix = inclusive - gathered
    if late is not None:
        prefix, late = lax.optimization_barrier((prefix, late))
    spread = lax.all_to_all(prefix, "seq", 0, 0, tiled=True)
    spread = spread.reshape(-1, width)[:size].reshape(own_total.shape)
    if early is None:
        return spread
    return spread, early, late


def lower_sum(own_total):
    return exclusive_scan(own_total, False)


def upper_sum(own_total, early, late):
    return exclusive_scan(own_total, True, early, late)


def body(query_raw, key_raw, value_raw, out_gain, out_grad):
    tok_rows, head_count, width = query_raw.shape
    blocks = tok_rows // GROUP
    blocked = (blocks, GROUP, head_count, width)
    query_act = jax.nn.silu(query_raw.astype(jnp.float32)).astype(jnp.bfloat16).reshape(blocked)
    key_act = jax.nn.silu(key_raw.astype(jnp.float32)).astype(jnp.bfloat16).reshape(blocked)
    value_blk = value_raw.reshape(blocked)
    mask = causal_mask(GROUP)[None, None]
    block_kv = jnp.einsum("cshd,cshe->chde", key_act, value_blk, preferred_element_type=jnp.float32)
    own_total = jnp.sum(block_kv, axis=0)
    before = lower_sum(own_total)
    if blocks == 1:
        state_b = lax.reduce_precision(before[None], 8, 7).astype(jnp.bfloat16)
    else:
        state_b = (before[None] + (jnp.cumsum(block_kv, axis=0) - block_kv)).astype(jnp.bfloat16)
    scores = jnp.einsum("cthd,cshd->chts", query_act, key_act, preferred_element_type=jnp.float32)
    attn = jnp.where(mask, scores, 0.0).astype(jnp.bfloat16)
    mixed = jnp.einsum("chts,cshe->cthe", attn, value_blk, preferred_element_type=jnp.float32)
    mixed = mixed + jnp.einsum(
        "cthd,chde->cthe", query_act, state_b, preferred_element_type=jnp.float32
    )
    mixed = mixed.reshape(tok_rows, head_count, width)
    grad_in = out_grad.astype(jnp.float32) * out_gain
    sq_part = jnp.sum(mixed * mixed, axis=(1, 2))
    cross_part = jnp.sum(grad_in * mixed, axis=(1, 2))
    both = jnp.stack([sq_part, cross_part])
    both = both + lax.ppermute(both, "head", [(0, 1), (1, 0)])
    sq_total, cross_total = both[0], both[1]
    features = head_count * width * lax.axis_size("head")
    inv_rms = lax.rsqrt(sq_total / features + 1e-06)
    delta_f32 = (
        grad_in * inv_rms[:, None, None]
        - mixed * (cross_total * inv_rms**3 / features)[:, None, None]
    )
    delta = delta_f32.astype(jnp.bfloat16)
    delta_blk = delta.reshape(blocked)
    block_grad = jnp.einsum(
        "cthd,cthe->chde", query_act.astype(jnp.float32), delta_f32.reshape(blocked),
        preferred_element_type=jnp.float32,
    )
    own_grad = jnp.sum(block_grad, axis=0)
    normed_out = (mixed * inv_rms[:, None, None] * out_gain).astype(jnp.bfloat16)
    after, delta_late, _ = upper_sum(own_grad, delta_blk, None)
    if blocks == 1:
        grad_state = lax.reduce_precision(after[None], 8, 7).astype(jnp.bfloat16)
    else:
        grad_state = (after[None] + (lax.cumsum(block_grad, axis=0, reverse=True) - block_grad)).astype(jnp.bfloat16)
    bscore = jnp.einsum("cthe,cshe->chts", delta_late, value_blk, preferred_element_type=jnp.float32)
    bscore = jnp.where(mask, bscore, 0.0).astype(jnp.bfloat16)
    dquery = jnp.einsum("chts,cshd->cthd", bscore, key_act, preferred_element_type=jnp.float32)
    dquery = dquery + jnp.einsum(
        "cthe,chde->cthd", delta_blk, state_b, preferred_element_type=jnp.float32
    )
    dkey = jnp.einsum("chts,cthd->cshd", bscore, query_act, preferred_element_type=jnp.float32)
    dkey = dkey + jnp.einsum(
        "cshe,chde->cshd", value_blk, grad_state, preferred_element_type=jnp.float32
    )
    dvalue = jnp.einsum("chts,cthe->cshe", attn, delta_blk, preferred_element_type=jnp.float32)
    dvalue = dvalue + jnp.einsum(
        "cshd,chde->cshe", key_act, grad_state, preferred_element_type=jnp.float32
    )
    whole = (tok_rows, head_count, width)
    query_grad = (dquery.reshape(whole) * silu_grad(query_raw.astype(jnp.float32))).astype(
        jnp.bfloat16
    )
    key_grad = (dkey.reshape(whole) * silu_grad(key_raw.astype(jnp.float32))).astype(jnp.bfloat16)
    value_grad = dvalue.reshape(whole).astype(jnp.bfloat16)
    return (normed_out, query_grad, key_grad, value_grad)


def solution(mesh):
    in_specs = (
        P("seq", "head", None),
        P("seq", "head", None),
        P("seq", "head", None),
        P("head", None),
        P("seq", "head", None),
    )
    out_specs = (
        P("seq", "head", None),
        P("seq", "head", None),
        P("seq", "head", None),
        P("seq", "head", None),
    )
    return jax.shard_map(body, mesh=mesh, in_specs=in_specs, out_specs=out_specs, check_vma=False)
```

```python
import jax
import jax.numpy as jnp
from jax import lax
from jax.sharding import PartitionSpec as P

GROUP = 256


def from_behind(shard, axis, by):
    count = lax.axis_size(axis)
    pairs = [(i, i + by) for i in range(count) if 0 <= i + by < count]
    return lax.ppermute(shard, axis, pairs)


def silu_grad(raw):
    sigma = jax.nn.sigmoid(raw)
    return sigma * (1.0 + raw * (1.0 - sigma))


def causal_mask(length):
    rows = lax.broadcasted_iota(jnp.int32, (length, length), 0)
    cols = lax.broadcasted_iota(jnp.int32, (length, length), 1)
    return cols <= rows


def exclusive_scan(own_total, reverse, early=None, late=None):
    count = lax.axis_size("seq")
    width = own_total.shape[-1]
    rows = own_total.reshape(-1, width)
    size = rows.shape[0]
    chunk = -(-size // count)
    rows = jnp.pad(rows, ((0, chunk * count - size), (0, 0)))
    gathered = lax.all_to_all(rows.reshape(count, chunk, width), "seq", 0, 0, tiled=True)
    if early is not None:
        gathered, early = lax.optimization_barrier((gathered, early))
    inclusive = lax.cumsum(gathered, axis=0)
    if reverse:
        prefix = inclusive[-1:] - inclusive
    else:
        prefix = inclusive - gathered
    if late is not None:
        prefix, late = lax.optimization_barrier((prefix, late))
    spread = lax.all_to_all(prefix, "seq", 0, 0, tiled=True)
    spread = spread.reshape(-1, width)[:size].reshape(own_total.shape)
    if early is None:
        return spread
    return spread, early, late


def lower_sum(own_total):
    return exclusive_scan(own_total, False)


def upper_sum(own_total, early, late):
    return exclusive_scan(own_total, True, early, late)


def body(query_raw, key_raw, value_raw, out_gain, out_grad):
    tok_rows, head_count, width = query_raw.shape
    blocks = tok_rows // GROUP
    blocked = (blocks, GROUP, head_count, width)
    query_act = jax.nn.silu(query_raw.astype(jnp.float32)).astype(jnp.bfloat16).reshape(blocked)
    key_act = jax.nn.silu(key_raw.astype(jnp.float32)).astype(jnp.bfloat16).reshape(blocked)
    value_blk = value_raw.reshape(blocked)
    mask = causal_mask(GROUP)[None, None]
    block_kv = jnp.einsum("cshd,cshe->chde", key_act, value_blk, preferred_element_type=jnp.float32)
    own_total = jnp.sum(block_kv, axis=0)
    before = lower_sum(own_total)
    if blocks == 1:
        state_b = lax.reduce_precision(before[None], 8, 7).astype(jnp.bfloat16)
    else:
        state_b = (before[None] + (jnp.cumsum(block_kv, axis=0) - block_kv)).astype(jnp.bfloat16)
    scores = jnp.einsum("cthd,cshd->chts", query_act, key_act, preferred_element_type=jnp.float32)
    attn = jnp.where(mask, scores, 0.0).astype(jnp.bfloat16)
    mixed = jnp.einsum("chts,cshe->cthe", attn, value_blk, preferred_element_type=jnp.float32)
    mixed = mixed + jnp.einsum(
        "cthd,chde->cthe", query_act, state_b, preferred_element_type=jnp.float32
    )
    mixed = mixed.reshape(tok_rows, head_count, width)
    grad_in = out_grad.astype(jnp.float32) * out_gain
    sq_part = jnp.sum(mixed * mixed, axis=(1, 2))
    cross_part = jnp.sum(grad_in * mixed, axis=(1, 2))
    both = jnp.stack([sq_part, cross_part])
    both = both + lax.ppermute(both, "head", [(0, 1), (1, 0)])
    sq_total, cross_total = both[0], both[1]
    features = head_count * width * lax.axis_size("head")
    inv_rms = lax.rsqrt(sq_total / features + 1e-06)
    delta = (
        grad_in * inv_rms[:, None, None]
        - mixed * (cross_total * inv_rms**3 / features)[:, None, None]
    ).astype(jnp.bfloat16)
    delta_blk = delta.reshape(blocked)
    block_grad = jnp.einsum(
        "cthd,cthe->chde", query_act, delta_blk, preferred_element_type=jnp.float32
    )
    own_grad = jnp.sum(block_grad, axis=0)
    normed_out = (mixed * inv_rms[:, None, None] * out_gain).astype(jnp.bfloat16)
    after, delta_late, _ = upper_sum(own_grad, delta_blk, None)
    if blocks == 1:
        grad_state = lax.reduce_precision(after[None], 8, 7).astype(jnp.bfloat16)
    else:
        grad_state = (after[None] + (lax.cumsum(block_grad, axis=0, reverse=True) - block_grad)).astype(jnp.bfloat16)
    bscore = jnp.einsum("cthe,cshe->chts", delta_late, value_blk, preferred_element_type=jnp.float32)
    bscore = jnp.where(mask, bscore, 0.0).astype(jnp.bfloat16)
    dquery = jnp.einsum("chts,cshd->cthd", bscore, key_act, preferred_element_type=jnp.float32)
    dquery = dquery + jnp.einsum(
        "cthe,chde->cthd", delta_blk, state_b, preferred_element_type=jnp.float32
    )
    dkey = jnp.einsum("chts,cthd->cshd", bscore, query_act, preferred_element_type=jnp.float32)
    dkey = dkey + jnp.einsum(
        "cshe,chde->cshd", value_blk, grad_state, preferred_element_type=jnp.float32
    )
    dvalue = jnp.einsum("chts,cthe->cshe", attn, delta_blk, preferred_element_type=jnp.float32)
    dvalue = dvalue + jnp.einsum(
        "cshd,chde->cshe", key_act, grad_state, preferred_element_type=jnp.float32
    )
    whole = (tok_rows, head_count, width)
    query_grad = (dquery.reshape(whole) * silu_grad(query_raw.astype(jnp.float32))).astype(
        jnp.bfloat16
    )
    key_grad = (dkey.reshape(whole) * silu_grad(key_raw.astype(jnp.float32))).astype(jnp.bfloat16)
    value_grad = dvalue.reshape(whole).astype(jnp.bfloat16)
    return (normed_out, query_grad, key_grad, value_grad)


def solution(mesh):
    in_specs = (
        P("seq", "head", None),
        P("seq", "head", None),
        P("seq", "head", None),
        P("head", None),
        P("seq", "head", None),
    )
    out_specs = (
        P("seq", "head", None),
        P("seq", "head", None),
        P("seq", "head", None),
        P("seq", "head", None),
    )
    return jax.shard_map(body, mesh=mesh, in_specs=in_specs, out_specs=out_specs, check_vma=False)
```

```python
import jax
import jax.numpy as jnp
from jax import lax
from jax.sharding import PartitionSpec as P

GROUP = 256


def from_behind(shard, axis, by):
    count = lax.axis_size(axis)
    pairs = [(i, i + by) for i in range(count) if 0 <= i + by < count]
    return lax.ppermute(shard, axis, pairs)


def silu_grad(raw):
    sigma = jax.nn.sigmoid(raw)
    return sigma * (1.0 + raw * (1.0 - sigma))


def causal_mask(length):
    rows = lax.broadcasted_iota(jnp.int32, (length, length), 0)
    cols = lax.broadcasted_iota(jnp.int32, (length, length), 1)
    return cols <= rows


def exclusive_scan(own_total, reverse, early=None, late=None):
    count = lax.axis_size("seq")
    width = own_total.shape[-1]
    rows = own_total.reshape(-1, width)
    size = rows.shape[0]
    chunk = -(-size // count)
    rows = jnp.pad(rows, ((0, chunk * count - size), (0, 0)))
    gathered = lax.all_to_all(rows.reshape(count, chunk, width), "seq", 0, 0, tiled=True)
    if early is not None:
        gathered, early = lax.optimization_barrier((gathered, early))
    inclusive = lax.cumsum(gathered, axis=0, reverse=reverse)
    prefix = inclusive - gathered
    if late is not None:
        prefix, late = lax.optimization_barrier((prefix, late))
    spread = lax.all_to_all(prefix, "seq", 0, 0, tiled=True)
    spread = spread.reshape(-1, width)[:size].reshape(own_total.shape)
    if early is None:
        return spread
    return spread, early, late


def lower_sum(own_total):
    return exclusive_scan(own_total, False)


def upper_sum(own_total, early, late):
    return exclusive_scan(own_total, True, early, late)


def body(query_raw, key_raw, value_raw, out_gain, out_grad):
    tok_rows, head_count, width = query_raw.shape
    blocks = tok_rows // GROUP
    blocked = (blocks, GROUP, head_count, width)
    query_act = jax.nn.silu(query_raw.astype(jnp.float32)).astype(jnp.bfloat16).reshape(blocked)
    key_act = jax.nn.silu(key_raw.astype(jnp.float32)).astype(jnp.bfloat16).reshape(blocked)
    value_blk = value_raw.reshape(blocked)
    mask = causal_mask(GROUP)[None, None]
    block_kv = jnp.einsum("cshe,cshd->ched", value_blk, key_act, preferred_element_type=jnp.float32)
    own_total = jnp.sum(block_kv, axis=0)
    before = lower_sum(own_total)
    if blocks == 1:
        state_b = lax.reduce_precision(before[None], 8, 7).astype(jnp.bfloat16)
    else:
        state_b = (before[None] + (jnp.cumsum(block_kv, axis=0) - block_kv)).astype(jnp.bfloat16)
    scores = jnp.einsum("cthd,cshd->chts", query_act, key_act, preferred_element_type=jnp.float32)
    attn = jnp.where(mask, scores, 0.0).astype(jnp.bfloat16)
    mixed = jnp.einsum("chts,cshe->cthe", attn, value_blk, preferred_element_type=jnp.float32)
    mixed = mixed + jnp.einsum(
        "cthd,ched->cthe", query_act, state_b, preferred_element_type=jnp.float32
    )
    mixed = mixed.reshape(tok_rows, head_count, width)
    grad_in = out_grad.astype(jnp.float32) * out_gain
    sq_part = jnp.sum(mixed * mixed, axis=(1, 2))
    cross_part = jnp.sum(grad_in * mixed, axis=(1, 2))
    both = jnp.stack([sq_part, cross_part])
    both = both + lax.ppermute(both, "head", [(0, 1), (1, 0)])
    sq_total, cross_total = both[0], both[1]
    features = head_count * width * lax.axis_size("head")
    inv_rms = lax.rsqrt(sq_total / features + 1e-06)
    delta = (
        grad_in * inv_rms[:, None, None]
        - mixed * (cross_total * inv_rms**3 / features)[:, None, None]
    ).astype(jnp.bfloat16)
    delta_blk = delta.reshape(blocked)
    block_grad = jnp.einsum(
        "cthd,cthe->chde", query_act, delta_blk, preferred_element_type=jnp.float32
    )
    own_grad = jnp.sum(block_grad, axis=0)
    normed_out = (mixed * inv_rms[:, None, None] * out_gain).astype(jnp.bfloat16)
    after, delta_late, _ = upper_sum(own_grad, delta_blk, None)
    if blocks == 1:
        grad_state = lax.reduce_precision(after[None], 8, 7).astype(jnp.bfloat16)
    else:
        grad_state = (after[None] + (lax.cumsum(block_grad, axis=0, reverse=True) - block_grad)).astype(jnp.bfloat16)
    bscore = jnp.einsum("cthe,cshe->chts", delta_late, value_blk, preferred_element_type=jnp.float32)
    bscore = jnp.where(mask, bscore, 0.0).astype(jnp.bfloat16)
    dquery = jnp.einsum("chts,cshd->cthd", bscore, key_act, preferred_element_type=jnp.float32)
    dquery = dquery + jnp.einsum(
        "cthe,ched->cthd", delta_blk, state_b, preferred_element_type=jnp.float32
    )
    dkey = jnp.einsum("chts,cthd->cshd", bscore, query_act, preferred_element_type=jnp.float32)
    dkey = dkey + jnp.einsum(
        "cshe,chde->cshd", value_blk, grad_state, preferred_element_type=jnp.float32
    )
    dvalue = jnp.einsum("chts,cthe->cshe", attn, delta_blk, preferred_element_type=jnp.float32)
    dvalue = dvalue + jnp.einsum(
        "cshd,chde->cshe", key_act, grad_state, preferred_element_type=jnp.float32
    )
    whole = (tok_rows, head_count, width)
    query_grad = (dquery.reshape(whole) * silu_grad(query_raw.astype(jnp.float32))).astype(
        jnp.bfloat16
    )
    key_grad = (dkey.reshape(whole) * silu_grad(key_raw.astype(jnp.float32))).astype(jnp.bfloat16)
    value_grad = dvalue.reshape(whole).astype(jnp.bfloat16)
    return (normed_out, query_grad, key_grad, value_grad)


def solution(mesh):
    in_specs = (
        P("seq", "head", None),
        P("seq", "head", None),
        P("seq", "head", None),
        P("head", None),
        P("seq", "head", None),
    )
    out_specs = (
        P("seq", "head", None),
        P("seq", "head", None),
        P("seq", "head", None),
        P("seq", "head", None),
    )
    return jax.shard_map(body, mesh=mesh, in_specs=in_specs, out_specs=out_specs, check_vma=False)
```

```python
import jax
import jax.numpy as jnp
from jax import lax
from jax.sharding import PartitionSpec as P

GROUP = 256


def from_behind(shard, axis, by):
    count = lax.axis_size(axis)
    pairs = [(i, i + by) for i in range(count) if 0 <= i + by < count]
    return lax.ppermute(shard, axis, pairs)


def silu_grad(raw):
    sigma = jax.nn.sigmoid(raw)
    return sigma * (1.0 + raw * (1.0 - sigma))


def causal_mask(length):
    rows = lax.broadcasted_iota(jnp.int32, (length, length), 0)
    cols = lax.broadcasted_iota(jnp.int32, (length, length), 1)
    return cols <= rows


def exclusive_scan(own_total, reverse, early=None, late=None):
    count = lax.axis_size("seq")
    width = own_total.shape[-1]
    rows = own_total.reshape(-1, width)
    size = rows.shape[0]
    chunk = -(-size // count)
    rows = jnp.pad(rows, ((0, chunk * count - size), (0, 0)))
    gathered = lax.all_to_all(rows.reshape(count, chunk, width), "seq", 0, 0, tiled=True)
    if early is not None:
        gathered, early = lax.optimization_barrier((gathered, early))
    inclusive = lax.cumsum(gathered, axis=0, reverse=reverse)
    prefix = inclusive - gathered
    if late is not None:
        prefix, late = lax.optimization_barrier((prefix, late))
    spread = lax.all_to_all(prefix, "seq", 0, 0, tiled=True)
    spread = spread.reshape(-1, width)[:size].reshape(own_total.shape)
    if early is None:
        return spread
    return spread, early, late


def lower_sum(own_total):
    return exclusive_scan(own_total, False)


def upper_sum(own_total, early, late):
    return exclusive_scan(own_total, True, early, late)


def body(query_raw, key_raw, value_raw, out_gain, out_grad):
    tok_rows, head_count, width = query_raw.shape
    blocks = tok_rows // GROUP
    blocked = (blocks, GROUP, head_count, width)
    query_act = jax.nn.silu(query_raw.astype(jnp.float32)).astype(jnp.bfloat16).reshape(blocked)
    key_act = jax.nn.silu(key_raw.astype(jnp.float32)).astype(jnp.bfloat16).reshape(blocked)
    value_blk = value_raw.reshape(blocked)
    mask = causal_mask(GROUP)[None, None]
    block_kv = jnp.einsum("cshe,cshd->ched", value_blk, key_act, preferred_element_type=jnp.float32)
    own_total = jnp.sum(block_kv, axis=0)
    before = lower_sum(own_total)
    if blocks == 1:
        state_b = lax.reduce_precision(before[None], 8, 7).astype(jnp.bfloat16)
    else:
        state_b = (before[None] + (jnp.cumsum(block_kv, axis=0) - block_kv)).astype(jnp.bfloat16)
    scores = jnp.einsum("cthd,cshd->chts", query_act, key_act, preferred_element_type=jnp.float32)
    attn = jnp.where(mask, scores, 0.0).astype(jnp.bfloat16)
    mixed = jnp.einsum("chts,cshe->cthe", attn, value_blk, preferred_element_type=jnp.float32)
    mixed = mixed + jnp.einsum(
        "cthd,ched->cthe", query_act, state_b, preferred_element_type=jnp.float32
    )
    mixed = mixed.reshape(tok_rows, head_count, width)
    grad_in = out_grad.astype(jnp.float32) * out_gain
    sq_part = jnp.sum(mixed * mixed, axis=(1, 2))
    cross_part = jnp.sum(grad_in * mixed, axis=(1, 2))
    both = jnp.stack([sq_part, cross_part])
    both = both + lax.ppermute(both, "head", [(0, 1), (1, 0)])
    sq_total, cross_total = both[0], both[1]
    features = head_count * width * lax.axis_size("head")
    inv_rms = lax.rsqrt(sq_total / features + 1e-06)
    delta_f32 = (
        grad_in * inv_rms[:, None, None]
        - mixed * (cross_total * inv_rms**3 / features)[:, None, None]
    )
    delta = delta_f32.astype(jnp.bfloat16)
    delta_blk = delta.reshape(blocked)
    block_grad = jnp.einsum(
        "cthd,cthe->chde", query_act.astype(jnp.float32), delta_f32.reshape(blocked),
        preferred_element_type=jnp.float32,
    )
    own_grad = jnp.sum(block_grad, axis=0)
    normed_out = (mixed * inv_rms[:, None, None] * out_gain).astype(jnp.bfloat16)
    after, delta_late, _ = upper_sum(own_grad, delta_blk, None)
    if blocks == 1:
        grad_state = lax.reduce_precision(after[None], 8, 7).astype(jnp.bfloat16)
    else:
        grad_state = (after[None] + (lax.cumsum(block_grad, axis=0, reverse=True) - block_grad)).astype(jnp.bfloat16)
    bscore = jnp.einsum("cthe,cshe->chts", delta_late, value_blk, preferred_element_type=jnp.float32)
    bscore = jnp.where(mask, bscore, 0.0).astype(jnp.bfloat16)
    dquery = jnp.einsum("chts,cshd->cthd", bscore, key_act, preferred_element_type=jnp.float32)
    dquery = dquery + jnp.einsum(
        "cthe,ched->cthd", delta_blk, state_b, preferred_element_type=jnp.float32
    )
    dkey = jnp.einsum("chts,cthd->cshd", bscore, query_act, preferred_element_type=jnp.float32)
    dkey = dkey + jnp.einsum(
        "cshe,chde->cshd", value_blk, grad_state, preferred_element_type=jnp.float32
    )
    dvalue = jnp.einsum("chts,cthe->cshe", attn, delta_blk, preferred_element_type=jnp.float32)
    dvalue = dvalue + jnp.einsum(
        "cshd,chde->cshe", key_act, grad_state, preferred_element_type=jnp.float32
    )
    whole = (tok_rows, head_count, width)
    query_grad = (dquery.reshape(whole) * silu_grad(query_raw.astype(jnp.float32))).astype(
        jnp.bfloat16
    )
    key_grad = (dkey.reshape(whole) * silu_grad(key_raw.astype(jnp.float32))).astype(jnp.bfloat16)
    value_grad = dvalue.reshape(whole).astype(jnp.bfloat16)
    return (normed_out, query_grad, key_grad, value_grad)


def solution(mesh):
    in_specs = (
        P("seq", "head", None),
        P("seq", "head", None),
        P("seq", "head", None),
        P("head", None),
        P("seq", "head", None),
    )
    out_specs = (
        P("seq", "head", None),
        P("seq", "head", None),
        P("seq", "head", None),
        P("seq", "head", None),
    )
    return jax.shard_map(body, mesh=mesh, in_specs=in_specs, out_specs=out_specs, check_vma=False)
```
